256 devices in a mesh: ctx: 32 (over x, z), tp: 8 (over y, core).
Axes of the slice: x: 4, y: 4, z: 8, core: 2. Of those that a mesh axis runs over, the one named last changes fastest.
Arguments:
- query_in: bfloat16 [16384, 4096], P('ctx', 'tp'), may hold values from -6 to 6
- key_in: bfloat16 [16384, 4096], P('ctx', 'tp'), may hold values from -6 to 6
- value_in: bfloat16 [16384, 4096], P('ctx', 'tp'), may hold values from -6 to 6
- out_grad: bfloat16 [16384, 4096], P('ctx', 'tp'), may hold values from -6 to 6
- doc_ids: int32 [16384], replicated, may hold values from 0 to 15, never falling along the last dimension, each value on 1 to 2048 neighbouring positions
- skip_gain: float32 [4096], P('tp'), may hold values from -4 to 4
- filter_taps: bfloat16 [2048, 8], P(('ctx', 'tp')), may hold values from -0.125 to 0.125
Outputs:
- mixed_out: bfloat16 [16384, 4096], P('ctx', 'tp')
- query_grad: bfloat16 [16384, 4096], P('ctx', 'tp')
- key_grad: bfloat16 [16384, 4096], P('ctx', 'tp')
- value_grad: bfloat16 [16384, 4096], P('ctx', 'tp')
- filter_grad: float32 [2048, 8], P(('ctx', 'tp'))
The draws below stay inside these ranges and needn't reach their ends.
Inputs may be any that keep to these rules, and one draw needn't show every extreme that they name: `doc_ids`: ids never fall along the tokens; each document is 1 to 2048 tokens long and one is exactly 2048 long.
All inputs are finite; a program needn't handle non-finite values.
Results may differ from the reference program's by a relative error of at most 0.0049.
Values may be sent and summed in bfloat16 or wider, within the bound.
No kernel may reach another device: no remote copies, remote signals or barrier semaphores. Data moves between devices by JAX's collectives and lax.ppermute only.
A program may use at most 128 MiB of HBM per device.

```python
import math
import jax
import jax.numpy as jnp
import numpy as np
from jax import lax

D = 4096
C = 256
MAXCH = 8
FGROUP = 512
FLEN = 2048
GROUPS = 8
TOKENS = 16384


def block_levels(stream_key, shape, split, low, largest):
    def one(position, blocks):
        steps = jax.random.uniform(jax.random.fold_in(jax.random.fold_in(stream_key, 6), position), (blocks,), jnp.float32, low / len(split), largest / len(split))
        return jnp.repeat(jnp.exp(steps), shape[position] // blocks).reshape((-1,) + (1,) * (len(shape) - position - 1))

    factor_of = one(*split[0])
    for cut in split[1:]:
        factor_of = factor_of * one(*cut)
    return factor_of


def length_profile(amount, total, most, skew):
    weights = [(1 << 20) // math.isqrt(rank ** skew) + 1 for rank in range(2, amount + 1)]
    surplus, counts = total - most - (amount - 1), [1] * (amount - 1)
    while surplus > 0:
        movable = [i for i in range(amount - 1) if counts[i] < most]
        mass, left = sum([weights[i] for i in movable]), surplus
        for i in movable:
            extra = min(most - counts[i], max(1, left * weights[i] // mass), surplus)
            counts[i] = counts[i] + extra
            surplus = surplus - extra
    return np.array([most] + counts)


def uneven(rng, count, total, limit, skew):
    if count == 2:
        one = jax.random.randint(rng, (), max(1, total - limit), min(limit, total - 1) + 1)
        return jnp.stack([one, total - one])
    tallies = jnp.asarray(length_profile(count, total, limit, skew), jnp.int32)
    pairs = (count - 1) // 2
    source_of, receiver = tallies[1:1 + 2 * pairs:2], tallies[2:2 + 2 * pairs:2]
    room = jnp.minimum(source_of - 1, limit - receiver)
    moved = jax.random.randint(jax.random.fold_in(rng, 1), (pairs,), 0, 1 << 20) % (room + 1)
    tallies = tallies.at[1:1 + 2 * pairs:2].set(source_of - moved).at[2:2 + 2 * pairs:2].set(receiver + moved)
    return tallies[jax.random.permutation(jax.random.fold_in(rng, 2), count)]


def gaussian(own_key, extent, deviation, most, pieces=(), held_as=jnp.bfloat16):
    level = block_levels(own_key, extent, pieces, -0.22, 0.18) if pieces else 1.0
    drawn = jax.random.normal(own_key, extent, jnp.float32) * deviation * level
    return jnp.minimum(jnp.maximum(drawn, -most), most).astype(held_as)


def setup_inputs(seed: int = 0) -> dict:
    key_list = jax.random.split(jax.random.key(seed), 8)
    query_in = gaussian(key_list[0], (TOKENS, D), 1.0, 6.0, ((0, 32), (1, 8)))
    key_in = gaussian(key_list[1], (TOKENS, D), 1.0, 6.0, ((0, 32), (1, 8)))
    value_in = gaussian(key_list[2], (TOKENS, D), 1.0, 6.0, ((0, 32), (1, 8)))
    out_grad = gaussian(key_list[3], (TOKENS, D), 1.0, 6.0, ((0, 32), (1, 8)))
    doc_ids = jnp.searchsorted(jnp.cumsum(uneven(key_list[4], 2 * TOKENS // FLEN, TOKENS, FLEN, 2)), jnp.arange(TOKENS), side="right").astype(jnp.int32)
    skip_gain = gaussian(key_list[5], (D,), 1.0, 4.0, ((0, 8),), jnp.float32)
    filter_taps = gaussian(key_list[6], (FLEN, GROUPS), FLEN ** -0.5, 0.125, ((0, 256),))
    return dict(query_in=query_in, key_in=key_in, value_in=value_in, out_grad=out_grad, doc_ids=doc_ids, skip_gain=skip_gain, filter_taps=filter_taps)


def shear_toeplitz(window, stretch):
    groups_n = window.shape[0]
    reverse = window[:, ::-1]
    repeated = jnp.tile(reverse, (1, stretch))
    repeated = repeated[:, :stretch * (2 * stretch - 1)].reshape(groups_n, stretch, 2 * stretch - 1)
    return repeated[:, :, stretch - 1:]

def diagonal_sums(matrix, stretch):
    groups_n = matrix.shape[0]
    flipped = matrix[:, :, ::-1]
    padded = jnp.concatenate([flipped, jnp.zeros_like(flipped)], axis=2)
    flat = padded.reshape(groups_n, 2 * stretch * stretch)[:, :stretch * (2 * stretch - 1)]
    return lax.optimization_barrier(jnp.sum(flat.reshape(groups_n, stretch, 2 * stretch - 1), axis=1))

def pair_mask(ids_reader, ids_source, base):
    stretch = ids_reader.shape[0]
    offset = base + jnp.arange(stretch, dtype=jnp.int32)[:, None] - jnp.arange(stretch, dtype=jnp.int32)[None, :]
    same = ids_reader[:, None] == ids_source[None, :]
    return jnp.where(same & (offset >= 0), 1.0, 0.0).astype(jnp.float32)

def reference(query_in, key_in, value_in, out_grad, doc_ids, skip_gain, filter_taps):
    stretches = TOKENS // C
    mixed_in = (key_in.astype(jnp.float32) * value_in.astype(jnp.float32)).astype(jnp.bfloat16)
    conv_grad = (out_grad.astype(jnp.float32) * query_in.astype(jnp.float32)).astype(jnp.bfloat16)
    sources = mixed_in.reshape(stretches, C, GROUPS, FGROUP)
    grads = conv_grad.reshape(stretches, C, GROUPS, FGROUP)
    segs = doc_ids.reshape(stretches, C)
    taps = filter_taps.T
    blank = jnp.zeros((GROUPS, C), taps.dtype)
    padded = jnp.concatenate([blank, taps, blank], axis=1)
    skip_four = skip_gain.reshape(GROUPS, FGROUP)
    state = skip_four * sources.astype(jnp.float32)
    behind = skip_four * grads.astype(jnp.float32)
    filter_ext = jnp.zeros((GROUPS, (MAXCH + 2) * C), jnp.float32)
    for lag in range(MAXCH + 1):
        tile = shear_toeplitz(padded[:, lag * C:lag * C + 2 * C], C).astype(jnp.float32)
        count = stretches - lag

        def one_pair(items, tile=tile, lag=lag):
            ids_reader, ids_source, source, grad = items
            mask = pair_mask(ids_reader, ids_source, lag * C)
            masked = tile * mask[None]
            source_f = source.astype(jnp.float32)
            grad_f = grad.astype(jnp.float32)
            ahead = jnp.einsum('gab,bgc->agc', masked, source_f, precision=lax.Precision.HIGHEST)
            back_term = jnp.einsum('gab,agc->bgc', masked, grad_f, precision=lax.Precision.HIGHEST)
            product = jnp.einsum('agc,bgc->gab', grad_f, source_f, precision=lax.Precision.HIGHEST) * mask[None]
            return (ahead, back_term, diagonal_sums(product, C))
        ahead, back_term, diags = lax.map(one_pair, (segs[lag:], segs[:count], sources[:count], grads[lag:]))
        state = state.at[lag:].add(ahead)
        behind = behind.at[:count].add(back_term)
        filter_ext = filter_ext.at[:, lag * C:lag * C + 2 * C - 1].add(lax.optimization_barrier(jnp.sum(diags, axis=0)))
    conv = state.reshape(TOKENS, D)
    mixed_out = (query_in.astype(jnp.float32) * conv).astype(jnp.bfloat16)
    query_grad = (out_grad.astype(jnp.float32) * conv).astype(jnp.bfloat16)
    mixed_grad = behind.reshape(TOKENS, D)
    key_grad = (mixed_grad * value_in.astype(jnp.float32)).astype(jnp.bfloat16)
    value_grad = (mixed_grad * key_in.astype(jnp.float32)).astype(jnp.bfloat16)
    scale = 1.0 / math.sqrt(FGROUP * TOKENS)
    filter_grad = (filter_ext[:, C - 1:C - 1 + FLEN] * scale).T
    return (mixed_out, query_grad, key_grad, value_grad, filter_grad)
```

```python
import math

import jax
import jax.numpy as jnp
from jax import lax
from jax.sharding import PartitionSpec as P

MAXCH = 8
FGROUP = 512
FLEN = 2048


def shifted(value, axis, steps):
    count = lax.axis_size(axis)
    leading, last = (max(0, -steps), min(count, count - steps))
    return lax.ppermute(value, axis, [(source, source + steps) for source in range(leading, last)])


def band(window, rows, cols):
    groups_n = window.shape[0]
    flat = jnp.tile(window, (1, rows))[:, : rows * cols]
    return flat.reshape(groups_n, rows, cols)


def shards(query_in, key_in, value_in, out_grad, doc_ids, skip_gain, filter_taps):
    rows, width = query_in.shape
    groups_here = width // FGROUP
    here = lax.axis_index("ctx")
    span = -(-FLEN // rows)
    hist = span * rows
    wide = hist + rows
    assert hist == FLEN

    full_taps = lax.all_gather(filter_taps, ("ctx", "tp"), axis=0, tiled=True)
    first_group = lax.axis_index("tp") * groups_here
    taps = lax.dynamic_slice_in_dim(full_taps, first_group, groups_here, axis=1).T

    mixed_in = (key_in.astype(jnp.float32) * value_in.astype(jnp.float32)).astype(jnp.bfloat16)
    conv_grad = (out_grad.astype(jnp.float32) * query_in.astype(jnp.float32)).astype(jnp.bfloat16)

    ahead = [mixed_in]
    behind = [conv_grad]
    for _ in range(span):
        ahead.append(shifted(ahead[-1], "ctx", 1))
        behind.append(shifted(behind[-1], "ctx", -1))
    sources = jnp.concatenate(ahead[::-1], axis=0).reshape(wide, groups_here, FGROUP)
    readers = jnp.concatenate(behind, axis=0).reshape(wide, groups_here, FGROUP)

    ids_pad = jnp.concatenate(
        [jnp.full((hist,), -1, jnp.int32), doc_ids, jnp.full((hist,), -2, jnp.int32)]
    )
    ids_own = lax.dynamic_slice_in_dim(doc_ids, here * rows, rows)
    ids_src = lax.dynamic_slice_in_dim(ids_pad, here * rows, wide)
    ids_rdr = lax.dynamic_slice_in_dim(ids_pad, here * rows + hist, wide)
    same_src = ids_own[:, None] == ids_src[None, :]
    same_rdr = ids_own[:, None] == ids_rdr[None, :]

    zero_taps = jnp.zeros((groups_here, wide + 1 - FLEN), taps.dtype)
    fwd_window = jnp.concatenate([zero_taps[:, :1], taps[:, ::-1], zero_taps[:, 1:]], axis=1)
    bwd_window = jnp.concatenate([taps, zero_taps], axis=1)
    fwd_tile = jnp.where(same_src[None], band(fwd_window, rows, wide), 0)
    bwd_tile = jnp.where(same_rdr[None], band(bwd_window, rows, wide), 0)

    skip = skip_gain.reshape(groups_here, FGROUP)
    own_src = mixed_in.reshape(rows, groups_here, FGROUP)
    own_grad = conv_grad.reshape(rows, groups_here, FGROUP)
    conv = skip * own_src.astype(jnp.float32) + jnp.einsum(
        "gab,bgc->agc", fwd_tile, sources, preferred_element_type=jnp.float32
    )
    mixed_grad = skip * own_grad.astype(jnp.float32) + jnp.einsum(
        "gab,bgc->agc", bwd_tile, readers, preferred_element_type=jnp.float32
    )
    product = jnp.einsum("agc,bgc->gab", own_grad, sources, preferred_element_type=jnp.float32)
    product = jnp.where(same_src[None], product, 0.0)
    skewed = jnp.pad(product.reshape(groups_here, rows * wide), ((0, 0), (0, rows)))
    diag = jnp.sum(skewed.reshape(groups_here, rows, wide + 1), axis=1)
    filter_part = diag[:, 1 : hist + 1][:, ::-1]

    conv = conv.reshape(rows, width)
    mixed_grad = mixed_grad.reshape(rows, width)
    mixed_out = (query_in.astype(jnp.float32) * conv).astype(jnp.bfloat16)
    query_grad = (out_grad.astype(jnp.float32) * conv).astype(jnp.bfloat16)
    key_grad = (mixed_grad * value_in.astype(jnp.float32)).astype(jnp.bfloat16)
    value_grad = (mixed_grad * key_in.astype(jnp.float32)).astype(jnp.bfloat16)

    placed = jnp.zeros((FLEN, full_taps.shape[1]), jnp.float32)
    placed = lax.dynamic_update_slice_in_dim(placed, filter_part.T, first_group, axis=1)
    summed = lax.psum_scatter(placed, ("ctx", "tp"), scatter_dimension=0, tiled=True)
    tokens = lax.axis_size("ctx") * rows
    filter_grad = summed * (1.0 / math.sqrt(FGROUP * tokens))
    return (mixed_out, query_grad, key_grad, value_grad, filter_grad)


def solution(mesh):
    in_specs = (
        P("ctx", "tp"),
        P("ctx", "tp"),
        P("ctx", "tp"),
        P("ctx", "tp"),
        P(),
        P("tp"),
        P(("ctx", "tp"), None),
    )
    out_specs = (
        P("ctx", "tp"),
        P("ctx", "tp"),
        P("ctx", "tp"),
        P("ctx", "tp"),
        P(("ctx", "tp"), None),
    )
    return jax.shard_map(shards, mesh=mesh, in_specs=in_specs, out_specs=out_specs, check_vma=False)
```

```python
import math

import jax
import jax.numpy as jnp
from jax import lax
from jax.experimental import pallas as pl
from jax.experimental.pallas import tpu as pltpu
from jax.sharding import PartitionSpec as P

MAXCH = 8
FGROUP = 512
FLEN = 2048
C = 256
INTERPRET = False


def shifted(value, axis, steps):
    count = lax.axis_size(axis)
    leading, last = (max(0, -steps), min(count, count - steps))
    return lax.ppermute(value, axis, [(source, source + steps) for source in range(leading, last)])


def swapped(value, axis, bit):
    count = lax.axis_size(axis)
    return lax.ppermute(value, axis, [(source, source ^ bit) for source in range(count)])


def gather_chunks(chunk, axis):
    here = lax.axis_index(axis)
    count = lax.axis_size(axis)
    held = chunk
    bit = 1
    while bit < count:
        other = swapped(held, axis, bit)
        upper = (here & bit) != 0
        held = jnp.concatenate([jnp.where(upper, other, held), jnp.where(upper, held, other)])
        bit *= 2
    return held


def scatter_sums(vector, axis):
    here = lax.axis_index(axis)
    count = lax.axis_size(axis)
    held = vector
    bit = count // 2
    while bit >= 1:
        half = held.shape[0] // 2
        low, high = held[:half], held[half:]
        upper = (here & bit) != 0
        other = swapped(jnp.where(upper, low, high), axis, bit)
        held = jnp.where(upper, high, low) + other
        bit //= 2
    return held


def conv_kernel(fwd_rows, bwd_rows, ids_own, ids_rev, ids_src, ids_rdr, skip, src, grads, grads_rev,
                conv_out, mgrad_out, filt_out, fwd_tiles, bwd_tiles):
    lags = MAXCH + 1
    own = src.shape[0] - MAXCH * C
    parts = own // C
    for lag in range(lags):
        wide = jnp.broadcast_to(fwd_rows[lag : lag + 1, :], (C, 2 * C))
        fwd_tiles[lag] = pltpu.roll(wide, 0, 1, stride=1, stride_axis=0)[:, C:].astype(jnp.bfloat16)
        wide = jnp.broadcast_to(bwd_rows[lag : lag + 1, :], (C, 2 * C))
        bwd_tiles[lag] = pltpu.roll(wide, 0, 1, stride=1, stride_axis=0)[:, C:].astype(jnp.bfloat16)
    skip_row = skip[...]
    sums = [jnp.zeros((1, 2 * C), jnp.float32) for _ in range(lags)]
    for r in range(parts):
        rows = slice(r * C, (r + 1) * C)
        reader_ids = ids_own[rows, :]
        reader_rev = ids_rev[rows, :]
        own_rows = slice(MAXCH * C + r * C, MAXCH * C + (r + 1) * C)
        acc = skip_row * src[own_rows, :].astype(jnp.float32)
        grad_rev = grads_rev[rows, :]
        for j in range(MAXCH + parts):
            lag = MAXCH + r - j
            if not 0 <= lag <= MAXCH:
                continue
            cols = slice(j * C, (j + 1) * C)
            block = src[cols, :]
            same = reader_ids == ids_src[:, cols]
            tile = jnp.where(same, fwd_tiles[lag], jnp.zeros((), jnp.bfloat16))
            acc = acc + jnp.dot(tile, block, preferred_element_type=jnp.float32)
            prod = lax.dot_general(grad_rev, block, (((1,), (1,)), ((), ())),
                                   preferred_element_type=jnp.float32)
            prod = jnp.where(reader_rev == ids_src[:, cols], prod, 0.0)
            wide = jnp.concatenate([prod, jnp.zeros((C, C), jnp.float32)], axis=1)
            wide = pltpu.roll(wide, 0, 1, stride=1, stride_axis=0)
            sums[lag] = sums[lag] + jnp.sum(wide, axis=0, keepdims=True)
        conv_out[rows, :] = acc
    for s in range(parts):
        rows = slice(s * C, (s + 1) * C)
        source_ids = ids_own[rows, :]
        acc = skip_row * grads[rows, :].astype(jnp.float32)
        for lag in range(lags):
            j = s + lag
            cols = slice(j * C, (j + 1) * C)
            same = source_ids == ids_rdr[:, cols]
            tile = jnp.where(same, bwd_tiles[lag], jnp.zeros((), jnp.bfloat16))
            acc = acc + jnp.dot(tile, grads[cols, :], preferred_element_type=jnp.float32)
        mgrad_out[rows, :] = acc
    for lag in range(lags):
        filt_out[lag : lag + 1, :] = sums[lag]


def local_conv(taps, ids_own, ids_src, ids_rdr, skip, src, grads):
    own, width = grads.shape[0] - MAXCH * C, grads.shape[1]
    lags = MAXCH + 1
    big = jnp.concatenate([jnp.zeros((2 * C,), jnp.float32), taps.astype(jnp.float32),
                           jnp.zeros((2 * C,), jnp.float32)])
    fwd_rows = jnp.stack([big[C * lag + C + 1 : C * lag + 3 * C + 1][::-1] for lag in range(lags)])
    bwd_rows = jnp.stack([big[C * lag + C : C * lag + 3 * C] for lag in range(lags)])
    parts = own // C
    ids_rev = ids_own.reshape(parts, C)[:, ::-1].reshape(own, 1)
    grads_rev = grads[:own].reshape(parts, C, width)[:, ::-1].reshape(own, width)
    conv, mgrad, sums = pl.pallas_call(
        conv_kernel,
        out_shape=(
            jax.ShapeDtypeStruct((own, width), jnp.float32),
            jax.ShapeDtypeStruct((own, width), jnp.float32),
            jax.ShapeDtypeStruct((lags, 2 * C), jnp.float32),
        ),
        scratch_shapes=[pltpu.VMEM((lags, C, C), jnp.bfloat16), pltpu.VMEM((lags, C, C), jnp.bfloat16)],
        compiler_params=pltpu.CompilerParams(vmem_limit_bytes=60 * 1024 * 1024),
        interpret=INTERPRET,
    )(fwd_rows, bwd_rows, ids_own.reshape(own, 1), ids_rev, ids_src.reshape(1, -1),
      ids_rdr.reshape(1, -1), skip.reshape(1, width), src, grads, grads_rev)
    ext = sum(
        jnp.pad(sums[lag, : 2 * C - 1][::-1], (C * lag + 1, (lags + 1) * C - C * lag - 2 * C))
        for lag in range(lags)
    )
    return conv, mgrad, ext[C : C + FLEN]


def shards(query_in, key_in, value_in, out_grad, doc_ids, skip_gain, filter_taps):
    rows, width = query_in.shape
    assert width == FGROUP and rows % C == 0
    here = lax.axis_index("ctx")
    span = -(-FLEN // rows)
    hist = span * rows
    assert hist == MAXCH * C

    pieces = lax.all_to_all(filter_taps, "tp", split_axis=1, concat_axis=0, tiled=True)
    taps = gather_chunks(pieces[:, 0], "ctx")

    mixed_in = (key_in.astype(jnp.float32) * value_in.astype(jnp.float32)).astype(jnp.bfloat16)
    conv_grad = (out_grad.astype(jnp.float32) * query_in.astype(jnp.float32)).astype(jnp.bfloat16)

    ahead = [mixed_in]
    behind = [conv_grad]
    for _ in range(span):
        ahead.append(shifted(ahead[-1], "ctx", 1))
        behind.append(shifted(behind[-1], "ctx", -1))
    sources = jnp.concatenate(ahead[::-1], axis=0)
    readers = jnp.concatenate(behind, axis=0)

    ids_pad = jnp.concatenate(
        [jnp.full((hist,), -1, jnp.int32), doc_ids, jnp.full((hist,), -2, jnp.int32)]
    )
    ids_own = lax.dynamic_slice_in_dim(doc_ids, here * rows, rows)
    ids_src = lax.dynamic_slice_in_dim(ids_pad, here * rows, hist + rows)
    ids_rdr = lax.dynamic_slice_in_dim(ids_pad, here * rows + hist, hist + rows)

    conv, mixed_grad, filter_part = local_conv(taps, ids_own, ids_src, ids_rdr, skip_gain, sources, readers)

    mixed_out = (query_in.astype(jnp.float32) * conv).astype(jnp.bfloat16)
    query_grad = (out_grad.astype(jnp.float32) * conv).astype(jnp.bfloat16)
    key_grad = (mixed_grad * value_in.astype(jnp.float32)).astype(jnp.bfloat16)
    value_grad = (mixed_grad * key_in.astype(jnp.float32)).astype(jnp.bfloat16)

    summed = scatter_sums(filter_part, "ctx")
    tokens = lax.axis_size("ctx") * rows
    scaled = (summed * (1.0 / math.sqrt(FGROUP * tokens)))[:, None]
    filter_grad = lax.all_to_all(scaled, "tp", split_axis=0, concat_axis=1, tiled=True)
    return (mixed_out, query_grad, key_grad, value_grad, filter_grad)


def solution(mesh):
    in_specs = (
        P("ctx", "tp"),
        P("ctx", "tp"),
        P("ctx", "tp"),
        P("ctx", "tp"),
        P(),
        P("tp"),
        P(("ctx", "tp"), None),
    )
    out_specs = (
        P("ctx", "tp"),
        P("ctx", "tp"),
        P("ctx", "tp"),
        P("ctx", "tp"),
        P(("ctx", "tp"), None),
    )
    return jax.shard_map(shards, mesh=mesh, in_specs=in_specs, out_specs=out_specs, check_vma=False)
```

```python
import math

import jax
import jax.numpy as jnp
from jax import lax
from jax.experimental import pallas as pl
from jax.experimental.pallas import tpu as pltpu
from jax.sharding import PartitionSpec as P

MAXCH = 8
FGROUP = 512
FLEN = 2048
C = 256
INTERPRET = False


def shifted(value, axis, steps):
    count = lax.axis_size(axis)
    leading, last = (max(0, -steps), min(count, count - steps))
    return lax.ppermute(value, axis, [(source, source + steps) for source in range(leading, last)])


def swapped(value, axis, bit):
    count = lax.axis_size(axis)
    return lax.ppermute(value, axis, [(source, source ^ bit) for source in range(count)])


def gather_chunks(chunk, axis):
    here = lax.axis_index(axis)
    count = lax.axis_size(axis)
    held = chunk
    bit = 1
    while bit < count:
        other = swapped(held, axis, bit)
        upper = (here & bit) != 0
        held = jnp.concatenate([jnp.where(upper, other, held), jnp.where(upper, held, other)])
        bit *= 2
    return held


def conv_kernel(fwd_rows, bwd_rows, ids_own, ids_rev, ids_src, ids_rdr, skip, *refs):
    lags = MAXCH + 1
    count = (len(refs) - 5) // 2
    src_refs, grad_refs = refs[:count], refs[count : 2 * count]
    conv_out, mgrad_out, filt_out, fwd_tiles, bwd_tiles = refs[2 * count :]
    own = src_refs[0].shape[0]
    parts = own // C

    def src(j):
        return src_refs[j // parts][(j % parts) * C : (j % parts + 1) * C, :]

    def grads(j):
        return grad_refs[j // parts][(j % parts) * C : (j % parts + 1) * C, :]

    exchange = (lax.broadcasted_iota(jnp.int32, (C, C), 0) + lax.broadcasted_iota(jnp.int32, (C, C), 1)
                == C - 1).astype(jnp.bfloat16)
    for lag in range(lags):
        wide = jnp.broadcast_to(fwd_rows[lag : lag + 1, :], (C, 2 * C))
        fwd_tiles[lag] = pltpu.roll(wide, 0, 1, stride=1, stride_axis=0)[:, C:].astype(jnp.bfloat16)
        wide = jnp.broadcast_to(bwd_rows[lag : lag + 1, :], (C, 2 * C))
        bwd_tiles[lag] = pltpu.roll(wide, 0, 1, stride=1, stride_axis=0)[:, C:].astype(jnp.bfloat16)
    skip_row = skip[...]
    sums = [jnp.zeros((1, 2 * C), jnp.float32) for _ in range(lags)]
    for r in range(parts):
        rows = slice(r * C, (r + 1) * C)
        reader_ids = ids_own[rows, :]
        reader_rev = ids_rev[rows, :]
        acc = skip_row * src(MAXCH + r).astype(jnp.float32)
        grad_rev = jnp.dot(exchange, grads(r), preferred_element_type=jnp.float32).astype(jnp.bfloat16)
        for j in range(MAXCH + parts):
            lag = MAXCH + r - j
            if not 0 <= lag <= MAXCH:
                continue
            cols = slice(j * C, (j + 1) * C)
            block = src(j)
            same = reader_ids == ids_src[:, cols]
            tile = jnp.where(same, fwd_tiles[lag], jnp.zeros((), jnp.bfloat16))
            acc = acc + jnp.dot(tile, block, preferred_element_type=jnp.float32)
            prod = lax.dot_general(grad_rev, block, (((1,), (1,)), ((), ())),
                                   preferred_element_type=jnp.float32)
            prod = jnp.where(reader_rev == ids_src[:, cols], prod, 0.0)
            wide = jnp.concatenate([prod, jnp.zeros((C, C), jnp.float32)], axis=1)
            wide = pltpu.roll(wide, 0, 1, stride=1, stride_axis=0)
            sums[lag] = sums[lag] + jnp.sum(wide, axis=0, keepdims=True)
        conv_out[rows, :] = acc
    for s in range(parts):
        rows = slice(s * C, (s + 1) * C)
        source_ids = ids_own[rows, :]
        acc = skip_row * grads(s).astype(jnp.float32)
        for lag in range(lags):
            j = s + lag
            cols = slice(j * C, (j + 1) * C)
            same = source_ids == ids_rdr[:, cols]
            tile = jnp.where(same, bwd_tiles[lag], jnp.zeros((), jnp.bfloat16))
            acc = acc + jnp.dot(tile, grads(j), preferred_element_type=jnp.float32)
        mgrad_out[rows, :] = acc
    for lag in range(lags):
        filt_out[lag : lag + 1, :] = sums[lag]


def local_conv(taps, ids_own, ids_src, ids_rdr, skip, src, grads):
    own, width = grads[0].shape
    lags = MAXCH + 1
    big = jnp.concatenate([jnp.zeros((2 * C,), jnp.float32), taps.astype(jnp.float32),
                           jnp.zeros((2 * C,), jnp.float32)])
    fwd_rows = jnp.stack([big[C * lag + C + 1 : C * lag + 3 * C + 1][::-1] for lag in range(lags)])
    bwd_rows = jnp.stack([big[C * lag + C : C * lag + 3 * C] for lag in range(lags)])
    parts = own // C
    ids_rev = ids_own.reshape(parts, C)[:, ::-1].reshape(own, 1)
    conv, mgrad, sums = pl.pallas_call(
        conv_kernel,
        out_shape=(
            jax.ShapeDtypeStruct((own, width), jnp.float32),
            jax.ShapeDtypeStruct((own, width), jnp.float32),
            jax.ShapeDtypeStruct((lags, 2 * C), jnp.float32),
        ),
        scratch_shapes=[pltpu.VMEM((lags, C, C), jnp.bfloat16), pltpu.VMEM((lags, C, C), jnp.bfloat16)],
        compiler_params=pltpu.CompilerParams(vmem_limit_bytes=60 * 1024 * 1024),
        interpret=INTERPRET,
    )(fwd_rows, bwd_rows, ids_own.reshape(own, 1), ids_rev, ids_src.reshape(1, -1),
      ids_rdr.reshape(1, -1), skip.reshape(1, width), *src, *grads)
    ext = sum(
        jnp.pad(sums[lag, : 2 * C - 1][::-1], (C * lag + 1, (lags + 1) * C - C * lag - 2 * C))
        for lag in range(lags)
    )
    return conv, mgrad, ext[C : C + FLEN]


def shards(query_in, key_in, value_in, out_grad, doc_ids, skip_gain, filter_taps):
    rows, width = query_in.shape
    assert width == FGROUP and rows % C == 0
    here = lax.axis_index("ctx")
    span = -(-FLEN // rows)
    hist = span * rows
    assert hist == MAXCH * C

    pieces = lax.all_to_all(filter_taps, "tp", split_axis=1, concat_axis=0, tiled=True)
    taps = gather_chunks(pieces[:, 0], "ctx")

    mixed_in = (key_in.astype(jnp.float32) * value_in.astype(jnp.float32)).astype(jnp.bfloat16)
    conv_grad = (out_grad.astype(jnp.float32) * query_in.astype(jnp.float32)).astype(jnp.bfloat16)

    ahead = [mixed_in]
    behind = [conv_grad]
    for _ in range(span):
        ahead.append(shifted(ahead[-1], "ctx", 1))
        behind.append(shifted(behind[-1], "ctx", -1))

    ids_pad = jnp.concatenate(
        [jnp.full((hist,), -1, jnp.int32), doc_ids, jnp.full((hist,), -2, jnp.int32)]
    )
    ids_own = lax.dynamic_slice_in_dim(doc_ids, here * rows, rows)
    ids_src = lax.dynamic_slice_in_dim(ids_pad, here * rows, hist + rows)
    ids_rdr = lax.dynamic_slice_in_dim(ids_pad, here * rows + hist, hist + rows)

    conv, mixed_grad, filter_part = local_conv(taps, ids_own, ids_src, ids_rdr, skip_gain, ahead[::-1], behind)

    mixed_out = (query_in.astype(jnp.float32) * conv).astype(jnp.bfloat16)
    query_grad = (out_grad.astype(jnp.float32) * conv).astype(jnp.bfloat16)
    key_grad = (mixed_grad * value_in.astype(jnp.float32)).astype(jnp.bfloat16)
    value_grad = (mixed_grad * key_in.astype(jnp.float32)).astype(jnp.bfloat16)

    every = ("ctx", "tp")
    devices = lax.axis_size(every)
    groups = lax.axis_size("tp")
    spread = lax.all_to_all(filter_part.reshape(devices, FLEN // devices), every, 0, 0, tiled=True)
    summed = jnp.sum(spread.reshape(devices // groups, groups, FLEN // devices), axis=0).T
    tokens = lax.axis_size("ctx") * rows
    filter_grad = summed * (1.0 / math.sqrt(FGROUP * tokens))
    return (mixed_out, query_grad, key_grad, value_grad, filter_grad)


def solution(mesh):
    in_specs = (
        P("ctx", "tp"),
        P("ctx", "tp"),
        P("ctx", "tp"),
        P("ctx", "tp"),
        P(),
        P("tp"),
        P(("ctx", "tp"), None),
    )
    out_specs = (
        P("ctx", "tp"),
        P("ctx", "tp"),
        P("ctx", "tp"),
        P("ctx", "tp"),
        P(("ctx", "tp"), None),
    )
    return jax.shard_map(shards, mesh=mesh, in_specs=in_specs, out_specs=out_specs, check_vma=False)
```

```python
import math

import jax
import jax.numpy as jnp
from jax import lax
from jax.experimental import pallas as pl
from jax.experimental.pallas import tpu as pltpu
from jax.sharding import PartitionSpec as P

MAXCH = 8
FGROUP = 512
FLEN = 2048
C = 256
INTERPRET = False


def shifted(value, axis, steps):
    count = lax.axis_size(axis)
    leading, last = (max(0, -steps), min(count, count - steps))
    return lax.ppermute(value, axis, [(source, source + steps) for source in range(leading, last)])


def band_tiles(rows_ref, tiles):
    for lag in range(MAXCH + 1):
        wide = jnp.broadcast_to(rows_ref[lag : lag + 1, :], (C, 2 * C))
        tiles[lag] = pltpu.roll(wide, 0, 1, stride=1, stride_axis=0)[:, C:].astype(jnp.bfloat16)


def filter_kernel(ids_rev, ids_src, *refs):
    lags = MAXCH + 1
    count = len(refs) - 2
    src_refs, grad_ref, filt_out = refs[:count], refs[count], refs[count + 1]
    own = grad_ref.shape[0]
    parts = own // C

    def src(j):
        return src_refs[j // parts][(j % parts) * C : (j % parts + 1) * C, :]

    exchange = (lax.broadcasted_iota(jnp.int32, (C, C), 0) + lax.broadcasted_iota(jnp.int32, (C, C), 1)
                == C - 1).astype(jnp.bfloat16)
    sums = [jnp.zeros((1, 2 * C), jnp.float32) for _ in range(lags)]
    for r in range(parts):
        reader_rev = ids_rev[r * C : (r + 1) * C, :]
        grad_rev = jnp.dot(exchange, grad_ref[r * C : (r + 1) * C, :],
                           preferred_element_type=jnp.float32).astype(jnp.bfloat16)
        for j in range(MAXCH + parts):
            lag = MAXCH + r - j
            if not 0 <= lag <= MAXCH:
                continue
            cols = slice(j * C, (j + 1) * C)
            prod = lax.dot_general(grad_rev, src(j), (((1,), (1,)), ((), ())),
                                   preferred_element_type=jnp.float32)
            prod = jnp.where(reader_rev == ids_src[:, cols], prod, 0.0)
            wide = jnp.concatenate([prod, jnp.zeros((C, C), jnp.float32)], axis=1)
            wide = pltpu.roll(wide, 0, 1, stride=1, stride_axis=0)
            sums[lag] = sums[lag] + jnp.sum(wide, axis=0, keepdims=True)
    for lag in range(lags):
        filt_out[lag : lag + 1, :] = sums[lag]


def conv_kernel(fwd_rows, bwd_rows, ids_own, ids_src, ids_rdr, skip, *refs):
    lags = MAXCH + 1
    count = (len(refs) - 4) // 2
    src_refs, grad_refs = refs[:count], refs[count : 2 * count]
    conv_out, mgrad_out, fwd_tiles, bwd_tiles = refs[2 * count :]
    own = src_refs[0].shape[0]
    parts = own // C

    def src(j):
        return src_refs[j // parts][(j % parts) * C : (j % parts + 1) * C, :]

    def grads(j):
        return grad_refs[j // parts][(j % parts) * C : (j % parts + 1) * C, :]

    band_tiles(fwd_rows, fwd_tiles)
    band_tiles(bwd_rows, bwd_tiles)
    skip_row = skip[...]
    for r in range(parts):
        reader_ids = ids_own[r * C : (r + 1) * C, :]
        acc = skip_row * src(MAXCH + r).astype(jnp.float32)
        for j in range(MAXCH + parts):
            lag = MAXCH + r - j
            if not 0 <= lag <= MAXCH:
                continue
            same = reader_ids == ids_src[:, j * C : (j + 1) * C]
            tile = jnp.where(same, fwd_tiles[lag], jnp.zeros((), jnp.bfloat16))
            acc = acc + jnp.dot(tile, src(j), preferred_element_type=jnp.float32)
        conv_out[r * C : (r + 1) * C, :] = acc
    for s in range(parts):
        source_ids = ids_own[s * C : (s + 1) * C, :]
        acc = skip_row * grads(s).astype(jnp.float32)
        for lag in range(lags):
            j = s + lag
            same = source_ids == ids_rdr[:, j * C : (j + 1) * C]
            tile = jnp.where(same, bwd_tiles[lag], jnp.zeros((), jnp.bfloat16))
            acc = acc + jnp.dot(tile, grads(j), preferred_element_type=jnp.float32)
        mgrad_out[s * C : (s + 1) * C, :] = acc


def filter_sums(ids_own, ids_src, src, grad):
    own = grad.shape[0]
    lags = MAXCH + 1
    parts = own // C
    ids_rev = ids_own.reshape(parts, C)[:, ::-1].reshape(own, 1)
    sums = pl.pallas_call(
        filter_kernel,
        out_shape=jax.ShapeDtypeStruct((lags, 2 * C), jnp.float32),
        compiler_params=pltpu.CompilerParams(vmem_limit_bytes=40 * 1024 * 1024),
        interpret=INTERPRET,
    )(ids_rev, ids_src.reshape(1, -1), *src, grad)
    ext = sum(
        jnp.pad(sums[lag, : 2 * C - 1][::-1], (C * lag + 1, (lags + 1) * C - C * lag - 2 * C))
        for lag in range(lags)
    )
    return ext[C : C + FLEN]


def local_conv(taps, ids_own, ids_src, ids_rdr, skip, src, grads):
    own, width = grads[0].shape
    lags = MAXCH + 1
    big = jnp.concatenate([jnp.zeros((2 * C,), jnp.float32), taps.astype(jnp.float32),
                           jnp.zeros((2 * C,), jnp.float32)])
    fwd_rows = jnp.stack([big[C * lag + C + 1 : C * lag + 3 * C + 1][::-1] for lag in range(lags)])
    bwd_rows = jnp.stack([big[C * lag + C : C * lag + 3 * C] for lag in range(lags)])
    return pl.pallas_call(
        conv_kernel,
        out_shape=(
            jax.ShapeDtypeStruct((own, width), jnp.float32),
            jax.ShapeDtypeStruct((own, width), jnp.float32),
        ),
        scratch_shapes=[pltpu.VMEM((lags, C, C), jnp.bfloat16), pltpu.VMEM((lags, C, C), jnp.bfloat16)],
        compiler_params=pltpu.CompilerParams(vmem_limit_bytes=60 * 1024 * 1024),
        interpret=INTERPRET,
    )(fwd_rows, bwd_rows, ids_own.reshape(own, 1), ids_src.reshape(1, -1),
      ids_rdr.reshape(1, -1), skip.reshape(1, width), *src, *grads)


def shards(query_in, key_in, value_in, out_grad, doc_ids, skip_gain, filter_taps):
    rows, width = query_in.shape
    assert width == FGROUP and rows % C == 0
    here = lax.axis_index("ctx")
    span = -(-FLEN // rows)
    hist = span * rows
    assert hist == MAXCH * C

    every = ("ctx", "tp")
    devices = lax.axis_size(every)
    groups = lax.axis_size("tp")
    offered = jnp.tile(filter_taps.T, (devices // groups, 1))
    taps = lax.all_to_all(offered, every, 0, 0, tiled=True).reshape(FLEN)

    mixed_in = (key_in.astype(jnp.float32) * value_in.astype(jnp.float32)).astype(jnp.bfloat16)
    conv_grad = (out_grad.astype(jnp.float32) * query_in.astype(jnp.float32)).astype(jnp.bfloat16)

    ahead = [mixed_in]
    behind = [conv_grad]
    for _ in range(span):
        ahead.append(shifted(ahead[-1], "ctx", 1))
        behind.append(shifted(behind[-1], "ctx", -1))

    ids_pad = jnp.concatenate(
        [jnp.full((hist,), -1, jnp.int32), doc_ids, jnp.full((hist,), -2, jnp.int32)]
    )
    ids_own = lax.dynamic_slice_in_dim(doc_ids, here * rows, rows)
    ids_src = lax.dynamic_slice_in_dim(ids_pad, here * rows, hist + rows)
    ids_rdr = lax.dynamic_slice_in_dim(ids_pad, here * rows + hist, hist + rows)

    filter_part = filter_sums(ids_own, ids_src, ahead[::-1], conv_grad)
    spread = lax.all_to_all(filter_part.reshape(devices, FLEN // devices), every, 0, 0, tiled=True)
    conv, mixed_grad = local_conv(taps, ids_own, ids_src, ids_rdr, skip_gain, ahead[::-1], behind)

    mixed_out = (query_in.astype(jnp.float32) * conv).astype(jnp.bfloat16)
    query_grad = (out_grad.astype(jnp.float32) * conv).astype(jnp.bfloat16)
    key_grad = (mixed_grad * value_in.astype(jnp.float32)).astype(jnp.bfloat16)
    value_grad = (mixed_grad * key_in.astype(jnp.float32)).astype(jnp.bfloat16)

    summed = jnp.sum(spread.reshape(devices // groups, groups, FLEN // devices), axis=0).T
    tokens = lax.axis_size("ctx") * rows
    filter_grad = summed * (1.0 / math.sqrt(FGROUP * tokens))
    return (mixed_out, query_grad, key_grad, value_grad, filter_grad)


def solution(mesh):
    in_specs = (
        P("ctx", "tp"),
        P("ctx", "tp"),
        P("ctx", "tp"),
        P("ctx", "tp"),
        P(),
        P("tp"),
        P(("ctx", "tp"), None),
    )
    out_specs = (
        P("ctx", "tp"),
        P("ctx", "tp"),
        P("ctx", "tp"),
        P("ctx", "tp"),
        P(("ctx", "tp"), None),
    )
    return jax.shard_map(shards, mesh=mesh, in_specs=in_specs, out_specs=out_specs, check_vma=False)
```

```python
import math

import jax
import jax.numpy as jnp
from jax import lax
from jax.experimental import pallas as pl
from jax.experimental.pallas import tpu as pltpu
from jax.sharding import PartitionSpec as P

MAXCH = 8
FGROUP = 512
FLEN = 2048
C = 256
INTERPRET = False


def shifted(value, axis, steps):
    count = lax.axis_size(axis)
    leading, last = (max(0, -steps), min(count, count - steps))
    return lax.ppermute(value, axis, [(source, source + steps) for source in range(leading, last)])


def band_tiles(taps_row, fwd_tiles, bwd_tiles):
    for lag in range(MAXCH + 1):
        start = C * lag + C
        wide = jnp.broadcast_to(taps_row[:, start : start + 2 * C], (C, 2 * C))
        tile = pltpu.roll(wide, 0, 1, stride=1, stride_axis=0)[:, C:]
        bwd_tiles[lag] = tile.astype(jnp.bfloat16)
        fwd_tiles[lag] = tile.T.astype(jnp.bfloat16)


def filter_kernel(ids_own, ids_rev, *refs):
    lags = MAXCH + 1
    count = len(refs) - 2
    src_refs, grad_ref, filt_out = refs[:count], refs[count], refs[count + 1]
    own = grad_ref.shape[0]
    parts = own // C

    exchange = (lax.broadcasted_iota(jnp.int32, (C, C), 0) + lax.broadcasted_iota(jnp.int32, (C, C), 1)
                == C - 1).astype(jnp.bfloat16)
    flipped = {}

    def src_rev(j):
        if j not in flipped:
            block = src_refs[j // parts][(j % parts) * C : (j % parts + 1) * C, :]
            flipped[j] = jnp.dot(exchange, block, preferred_element_type=jnp.float32).astype(jnp.bfloat16)
        return flipped[j]

    sums = [jnp.zeros((1, 2 * C), jnp.float32) for _ in range(lags)]
    for r in range(parts):
        reader_ids = ids_own[r * C : (r + 1) * C, :]
        grad = grad_ref[r * C : (r + 1) * C, :]
        for j in range(MAXCH + parts):
            lag = MAXCH + r - j
            if not 0 <= lag <= MAXCH:
                continue
            prod = lax.dot_general(grad, src_rev(j), (((1,), (1,)), ((), ())),
                                   preferred_element_type=jnp.float32)
            prod = jnp.where(reader_ids == ids_rev[:, j * C : (j + 1) * C], prod, 0.0)
            wide = jnp.concatenate([prod, jnp.zeros((C, C), jnp.float32)], axis=1)
            wide = pltpu.roll(wide, 0, 1, stride=1, stride_axis=0)
            sums[lag] = sums[lag] + jnp.sum(wide, axis=0, keepdims=True)
    filt_out[...] = jnp.zeros(filt_out.shape, jnp.float32)
    for lag in range(lags):
        filt_out[:, C * lag : C * lag + 2 * C] += sums[lag]


def conv_kernel(taps_row, ids_own, ids_src, ids_rdr, skip, *refs):
    lags = MAXCH + 1
    count = (len(refs) - 4) // 2
    src_refs, grad_refs = refs[:count], refs[count : 2 * count]
    conv_out, mgrad_out, fwd_tiles, bwd_tiles = refs[2 * count :]
    own = src_refs[0].shape[0]
    parts = own // C

    def src(j):
        return src_refs[j // parts][(j % parts) * C : (j % parts + 1) * C, :]

    def grads(j):
        return grad_refs[j // parts][(j % parts) * C : (j % parts + 1) * C, :]

    band_tiles(taps_row, fwd_tiles, bwd_tiles)
    skip_row = skip[...]
    for r in range(parts):
        reader_ids = ids_own[r * C : (r + 1) * C, :]
        acc = skip_row * src(MAXCH + r).astype(jnp.float32)
        for j in range(MAXCH + parts):
            lag = MAXCH + r - j
            if not 0 <= lag <= MAXCH:
                continue
            same = reader_ids == ids_src[:, j * C : (j + 1) * C]
            tile = jnp.where(same, fwd_tiles[lag], jnp.zeros((), jnp.bfloat16))
            acc = acc + jnp.dot(tile, src(j), preferred_element_type=jnp.float32)
        conv_out[r * C : (r + 1) * C, :] = acc
    for s in range(parts):
        source_ids = ids_own[s * C : (s + 1) * C, :]
        acc = skip_row * grads(s).astype(jnp.float32)
        for lag in range(lags):
            j = s + lag
            same = source_ids == ids_rdr[:, j * C : (j + 1) * C]
            tile = jnp.where(same, bwd_tiles[lag], jnp.zeros((), jnp.bfloat16))
            acc = acc + jnp.dot(tile, grads(j), preferred_element_type=jnp.float32)
        mgrad_out[s * C : (s + 1) * C, :] = acc


def filter_sums(ids_own, ids_src, src, grad):
    own = grad.shape[0]
    blocks = ids_src.shape[0] // C
    ids_rev = ids_src.reshape(blocks, C)[:, ::-1].reshape(1, blocks * C)
    ext = pl.pallas_call(
        filter_kernel,
        out_shape=jax.ShapeDtypeStruct((1, (MAXCH + 2) * C), jnp.float32),
        compiler_params=pltpu.CompilerParams(vmem_limit_bytes=40 * 1024 * 1024),
        interpret=INTERPRET,
    )(ids_own.reshape(own, 1), ids_rev, *src, grad)
    return ext[0, C - 1 : C - 1 + FLEN]


def local_conv(taps, ids_own, ids_src, ids_rdr, skip, src, grads):
    own, width = grads[0].shape
    lags = MAXCH + 1
    taps_row = jnp.pad(taps.astype(jnp.float32), (2 * C, 2 * C)).reshape(1, -1)
    return pl.pallas_call(
        conv_kernel,
        out_shape=(
            jax.ShapeDtypeStruct((own, width), jnp.float32),
            jax.ShapeDtypeStruct((own, width), jnp.float32),
        ),
        scratch_shapes=[pltpu.VMEM((lags, C, C), jnp.bfloat16), pltpu.VMEM((lags, C, C), jnp.bfloat16)],
        compiler_params=pltpu.CompilerParams(vmem_limit_bytes=60 * 1024 * 1024),
        interpret=INTERPRET,
    )(taps_row, ids_own.reshape(own, 1), ids_src.reshape(1, -1),
      ids_rdr.reshape(1, -1), skip.reshape(1, width), *src, *grads)


def shards(query_in, key_in, value_in, out_grad, doc_ids, skip_gain, filter_taps):
    rows, width = query_in.shape
    assert width == FGROUP and rows % C == 0
    here = lax.axis_index("ctx")
    span = -(-FLEN // rows)
    hist = span * rows
    assert hist == MAXCH * C

    every = ("ctx", "tp")
    devices = lax.axis_size(every)
    groups = lax.axis_size("tp")
    offered = jnp.tile(filter_taps.T, (devices // groups, 1))
    taps = lax.all_to_all(offered, every, 0, 0, tiled=True).reshape(FLEN)

    mixed_in = (key_in.astype(jnp.float32) * value_in.astype(jnp.float32)).astype(jnp.bfloat16)
    conv_grad = (out_grad.astype(jnp.float32) * query_in.astype(jnp.float32)).astype(jnp.bfloat16)

    ahead = [mixed_in]
    behind = [conv_grad]
    for _ in range(span):
        ahead.append(shifted(ahead[-1], "ctx", 1))
        behind.append(shifted(behind[-1], "ctx", -1))

    ids_pad = jnp.concatenate(
        [jnp.full((hist,), -1, jnp.int32), doc_ids, jnp.full((hist,), -2, jnp.int32)]
    )
    ids_own = lax.dynamic_slice_in_dim(doc_ids, here * rows, rows)
    ids_src = lax.dynamic_slice_in_dim(ids_pad, here * rows, hist + rows)
    ids_rdr = lax.dynamic_slice_in_dim(ids_pad, here * rows + hist, hist + rows)

    filter_part = filter_sums(ids_own, ids_src, ahead[::-1], conv_grad)
    spread = lax.all_to_all(filter_part.reshape(devices, FLEN // devices), every, 0, 0, tiled=True)
    conv, mixed_grad = local_conv(taps, ids_own, ids_src, ids_rdr, skip_gain, ahead[::-1], behind)

    mixed_out = (query_in.astype(jnp.float32) * conv).astype(jnp.bfloat16)
    query_grad = (out_grad.astype(jnp.float32) * conv).astype(jnp.bfloat16)
    key_grad = (mixed_grad * value_in.astype(jnp.float32)).astype(jnp.bfloat16)
    value_grad = (mixed_grad * key_in.astype(jnp.float32)).astype(jnp.bfloat16)

    summed = jnp.sum(spread.reshape(devices // groups, groups, FLEN // devices), axis=0).T
    tokens = lax.axis_size("ctx") * rows
    filter_grad = summed * (1.0 / math.sqrt(FGROUP * tokens))
    return (mixed_out, query_grad, key_grad, value_grad, filter_grad)


def solution(mesh):
    in_specs = (
        P("ctx", "tp"),
        P("ctx", "tp"),
        P("ctx", "tp"),
        P("ctx", "tp"),
        P(),
        P("tp"),
        P(("ctx", "tp"), None),
    )
    out_specs = (
        P("ctx", "tp"),
        P("ctx", "tp"),
        P("ctx", "tp"),
        P("ctx", "tp"),
        P(("ctx", "tp"), None),
    )
    return jax.shard_map(shards, mesh=mesh, in_specs=in_specs, out_specs=out_specs, check_vma=False)
```

```python
import math

import jax
import jax.numpy as jnp
from jax import lax
from jax.experimental import pallas as pl
from jax.experimental.pallas import tpu as pltpu
from jax.sharding import PartitionSpec as P

MAXCH = 8
FGROUP = 512
FLEN = 2048
C = 256
INTERPRET = False


def shifted(value, axis, steps):
    count = lax.axis_size(axis)
    leading, last = (max(0, -steps), min(count, count - steps))
    return lax.ppermute(value, axis, [(source, source + steps) for source in range(leading, last)])


def band_tiles(taps_row, fwd_tiles, bwd_tiles):
    for lag in range(MAXCH + 1):
        start = C * lag + C
        wide = jnp.broadcast_to(taps_row[:, start : start + 2 * C], (C, 2 * C))
        tile = pltpu.roll(wide, 0, 1, stride=1, stride_axis=0)[:, C:]
        bwd_tiles[lag] = tile.astype(jnp.bfloat16)
        fwd_tiles[lag] = tile.T.astype(jnp.bfloat16)


def filter_kernel(ids_own, ids_rev, *refs):
    lags = MAXCH + 1
    count = len(refs) - 2
    src_refs, grad_ref, filt_out = refs[:count], refs[count], refs[count + 1]
    own = grad_ref.shape[0]
    parts = own // C

    exchange = (lax.broadcasted_iota(jnp.int32, (C, C), 0) + lax.broadcasted_iota(jnp.int32, (C, C), 1)
                == C - 1).astype(jnp.bfloat16)
    flipped = {}

    def src_rev(j):
        if j not in flipped:
            block = src_refs[j // parts][(j % parts) * C : (j % parts + 1) * C, :]
            flipped[j] = jnp.dot(exchange, block, preferred_element_type=jnp.float32).astype(jnp.bfloat16)
        return flipped[j]

    sums = [jnp.zeros((1, 2 * C), jnp.float32) for _ in range(lags)]
    for r in range(parts):
        reader_ids = ids_own[r * C : (r + 1) * C, :]
        grad = grad_ref[r * C : (r + 1) * C, :]
        for j in range(MAXCH + parts):
            lag = MAXCH + r - j
            if not 0 <= lag <= MAXCH:
                continue
            prod = lax.dot_general(grad, src_rev(j), (((1,), (1,)), ((), ())),
                                   preferred_element_type=jnp.float32)
            prod = jnp.where(reader_ids == ids_rev[:, j * C : (j + 1) * C], prod, 0.0)
            wide = jnp.concatenate([prod, jnp.zeros((C, C), jnp.float32)], axis=1)
            wide = pltpu.roll(wide, 0, 1, stride=1, stride_axis=0)
            sums[lag] = sums[lag] + jnp.sum(wide, axis=0, keepdims=True)
    filt_out[...] = jnp.zeros(filt_out.shape, jnp.float32)
    for lag in range(lags):
        filt_out[:, C * lag : C * lag + 2 * C] += sums[lag]


def conv_kernel(taps_row, ids_own, ids_src, ids_rdr, skip, *refs):
    lags = MAXCH + 1
    count = (len(refs) - 4) // 2
    src_refs, grad_refs = refs[:count], refs[count : 2 * count]
    conv_out, mgrad_out, fwd_tiles, bwd_tiles = refs[2 * count :]
    own = src_refs[0].shape[0]
    parts = own // C

    def src(j):
        return src_refs[j // parts][(j % parts) * C : (j % parts + 1) * C, :]

    def grads(j):
        return grad_refs[j // parts][(j % parts) * C : (j % parts + 1) * C, :]

    band_tiles(taps_row, fwd_tiles, bwd_tiles)
    skip_row = skip[...]
    for r in range(parts):
        reader_ids = ids_own[r * C : (r + 1) * C, :]
        acc = skip_row * src(MAXCH + r).astype(jnp.float32)
        for j in range(MAXCH + parts):
            lag = MAXCH + r - j
            if not 0 <= lag <= MAXCH:
                continue
            same = reader_ids == ids_src[:, j * C : (j + 1) * C]
            tile = jnp.where(same, fwd_tiles[lag], jnp.zeros((), jnp.bfloat16))
            acc = acc + jnp.dot(tile, src(j), preferred_element_type=jnp.float32)
        conv_out[r * C : (r + 1) * C, :] = acc
    for s in range(parts):
        source_ids = ids_own[s * C : (s + 1) * C, :]
        acc = skip_row * grads(s).astype(jnp.float32)
        for lag in range(lags):
            j = s + lag
            same = source_ids == ids_rdr[:, j * C : (j + 1) * C]
            tile = jnp.where(same, bwd_tiles[lag], jnp.zeros((), jnp.bfloat16))
            acc = acc + jnp.dot(tile, grads(j), preferred_element_type=jnp.float32)
        mgrad_out[s * C : (s + 1) * C, :] = acc


def filter_sums(ids_own, ids_src, src, grad):
    own = grad.shape[0]
    blocks = ids_src.shape[0] // C
    ids_rev = ids_src.reshape(blocks, C)[:, ::-1].reshape(1, blocks * C)
    ext = pl.pallas_call(
        filter_kernel,
        out_shape=jax.ShapeDtypeStruct((1, (MAXCH + 2) * C), jnp.float32),
        compiler_params=pltpu.CompilerParams(vmem_limit_bytes=40 * 1024 * 1024),
        interpret=INTERPRET,
    )(ids_own.reshape(own, 1), ids_rev, *src, grad)
    return ext[0, C - 1 : C - 1 + FLEN]


def local_conv(taps, ids_own, ids_src, ids_rdr, skip, src, grads):
    own, width = grads[0].shape
    lags = MAXCH + 1
    taps_row = jnp.pad(taps.astype(jnp.float32), (2 * C, 2 * C)).reshape(1, -1)
    return pl.pallas_call(
        conv_kernel,
        out_shape=(
            jax.ShapeDtypeStruct((own, width), jnp.float32),
            jax.ShapeDtypeStruct((own, width), jnp.float32),
        ),
        scratch_shapes=[pltpu.VMEM((lags, C, C), jnp.bfloat16), pltpu.VMEM((lags, C, C), jnp.bfloat16)],
        compiler_params=pltpu.CompilerParams(vmem_limit_bytes=60 * 1024 * 1024),
        interpret=INTERPRET,
    )(taps_row, ids_own.reshape(own, 1), ids_src.reshape(1, -1),
      ids_rdr.reshape(1, -1), skip.reshape(1, width), *src, *grads)


def shards(query_in, key_in, value_in, out_grad, doc_ids, skip_gain, filter_taps):
    rows, width = query_in.shape
    assert width == FGROUP and rows % C == 0
    here = lax.axis_index("ctx")
    span = -(-FLEN // rows)
    hist = span * rows
    assert hist == MAXCH * C

    every = ("ctx", "tp")
    devices = lax.axis_size(every)
    groups = lax.axis_size("tp")
    offered = jnp.tile(filter_taps.T, (devices // groups, 1))
    taps = lax.all_to_all(offered, every, 0, 0, tiled=True).reshape(FLEN)

    mixed_in = (key_in.astype(jnp.float32) * value_in.astype(jnp.float32)).astype(jnp.bfloat16)
    conv_grad = (out_grad.astype(jnp.float32) * query_in.astype(jnp.float32)).astype(jnp.bfloat16)

    ahead = [mixed_in]
    behind = [conv_grad]
    for step in range(span):
        ahead.append(shifted(ahead[-1], "ctx", 1))
        behind.append(shifted(behind[-1], "ctx", -1))
        if step == 0:
            ahead[-1], behind[-1], taps = lax.optimization_barrier((ahead[-1], behind[-1], taps))

    ids_pad = jnp.concatenate(
        [jnp.full((hist,), -1, jnp.int32), doc_ids, jnp.full((hist,), -2, jnp.int32)]
    )
    ids_own = lax.dynamic_slice_in_dim(doc_ids, here * rows, rows)
    ids_src = lax.dynamic_slice_in_dim(ids_pad, here * rows, hist + rows)
    ids_rdr = lax.dynamic_slice_in_dim(ids_pad, here * rows + hist, hist + rows)

    filter_part = filter_sums(ids_own, ids_src, ahead[::-1], conv_grad)
    conv, mixed_grad = local_conv(taps, ids_own, ids_src, ids_rdr, skip_gain, ahead[::-1], behind)

    mixed_out = (query_in.astype(jnp.float32) * conv).astype(jnp.bfloat16)
    query_grad = (out_grad.astype(jnp.float32) * conv).astype(jnp.bfloat16)
    key_grad = (mixed_grad * value_in.astype(jnp.float32)).astype(jnp.bfloat16)
    value_grad = (mixed_grad * key_in.astype(jnp.float32)).astype(jnp.bfloat16)
    filter_part, mixed_out, query_grad, key_grad, value_grad = lax.optimization_barrier(
        (filter_part, mixed_out, query_grad, key_grad, value_grad))
    spread = lax.all_to_all(filter_part.reshape(devices, FLEN // devices), every, 0, 0, tiled=True)

    summed = jnp.sum(spread.reshape(devices // groups, groups, FLEN // devices), axis=0).T
    tokens = lax.axis_size("ctx") * rows
    filter_grad = summed * (1.0 / math.sqrt(FGROUP * tokens))
    return (mixed_out, query_grad, key_grad, value_grad, filter_grad)


def solution(mesh):
    in_specs = (
        P("ctx", "tp"),
        P("ctx", "tp"),
        P("ctx", "tp"),
        P("ctx", "tp"),
        P(),
        P("tp"),
        P(("ctx", "tp"), None),
    )
    out_specs = (
        P("ctx", "tp"),
        P("ctx", "tp"),
        P("ctx", "tp"),
        P("ctx", "tp"),
        P(("ctx", "tp"), None),
    )
    return jax.shard_map(shards, mesh=mesh, in_specs=in_specs, out_specs=out_specs, check_vma=False)
```

```python
import math

import jax
import jax.numpy as jnp
from jax import lax
from jax.experimental import pallas as pl
from jax.experimental.pallas import tpu as pltpu
from jax.sharding import PartitionSpec as P

MAXCH = 8
FGROUP = 512
FLEN = 2048
C = 256
INTERPRET = False


def shifted(value, axis, steps):
    count = lax.axis_size(axis)
    leading, last = (max(0, -steps), min(count, count - steps))
    return lax.ppermute(value, axis, [(source, source + steps) for source in range(leading, last)])


def band_tiles(taps_row, fwd_tiles, bwd_tiles):
    for lag in range(MAXCH + 1):
        start = C * lag + C
        wide = jnp.broadcast_to(taps_row[:, start : start + 2 * C], (C, 2 * C))
        tile = pltpu.roll(wide, 0, 1, stride=1, stride_axis=0)[:, C:]
        bwd_tiles[lag] = tile.astype(jnp.bfloat16)
        fwd_tiles[lag] = tile.T.astype(jnp.bfloat16)


def filter_kernel(ids_own, ids_rev, *refs):
    lags = MAXCH + 1
    count = len(refs) - 2
    src_refs, grad_ref, filt_out = refs[:count], refs[count], refs[count + 1]
    own = grad_ref.shape[0]
    parts = own // C

    exchange = (lax.broadcasted_iota(jnp.int32, (C, C), 0) + lax.broadcasted_iota(jnp.int32, (C, C), 1)
                == C - 1).astype(jnp.bfloat16)
    flipped = {}

    def src_rev(j):
        if j not in flipped:
            block = src_refs[j // parts][(j % parts) * C : (j % parts + 1) * C, :]
            flipped[j] = jnp.dot(exchange, block, preferred_element_type=jnp.float32).astype(jnp.bfloat16)
        return flipped[j]

    sums = [jnp.zeros((1, 2 * C), jnp.float32) for _ in range(lags)]
    for r in range(parts):
        reader_ids = ids_own[r * C : (r + 1) * C, :]
        grad = grad_ref[r * C : (r + 1) * C, :]
        for j in range(MAXCH + parts):
            lag = MAXCH + r - j
            if not 0 <= lag <= MAXCH:
                continue
            prod = lax.dot_general(grad, src_rev(j), (((1,), (1,)), ((), ())),
                                   preferred_element_type=jnp.float32)
            prod = jnp.where(reader_ids == ids_rev[:, j * C : (j + 1) * C], prod, 0.0)
            wide = jnp.concatenate([prod, jnp.zeros((C, C), jnp.float32)], axis=1)
            wide = pltpu.roll(wide, 0, 1, stride=1, stride_axis=0)
            sums[lag] = sums[lag] + jnp.sum(wide, axis=0, keepdims=True)
    filt_out[...] = jnp.zeros(filt_out.shape, jnp.float32)
    for lag in range(lags):
        filt_out[:, C * lag : C * lag + 2 * C] += sums[lag]


def conv_kernel(taps_row, ids_own, ids_src, ids_rdr, skip, *refs):
    lags = MAXCH + 1
    count = (len(refs) - 4) // 2
    src_refs, grad_refs = refs[:count], refs[count : 2 * count]
    conv_out, mgrad_out, fwd_tiles, bwd_tiles = refs[2 * count :]
    own = src_refs[0].shape[0]
    parts = own // C

    def src(j):
        return src_refs[j // parts][(j % parts) * C : (j % parts + 1) * C, :]

    def grads(j):
        return grad_refs[j // parts][(j % parts) * C : (j % parts + 1) * C, :]

    band_tiles(taps_row, fwd_tiles, bwd_tiles)
    skip_row = skip[...]
    for r in range(parts):
        reader_ids = ids_own[r * C : (r + 1) * C, :]
        acc = skip_row * src(MAXCH + r).astype(jnp.float32)
        for j in range(MAXCH + parts):
            lag = MAXCH + r - j
            if not 0 <= lag <= MAXCH:
                continue
            same = reader_ids == ids_src[:, j * C : (j + 1) * C]
            tile = jnp.where(same, fwd_tiles[lag], jnp.zeros((), jnp.bfloat16))
            acc = acc + jnp.dot(tile, src(j), preferred_element_type=jnp.float32)
        conv_out[r * C : (r + 1) * C, :] = acc
    for s in range(parts):
        source_ids = ids_own[s * C : (s + 1) * C, :]
        acc = skip_row * grads(s).astype(jnp.float32)
        for lag in range(lags):
            j = s + lag
            same = source_ids == ids_rdr[:, j * C : (j + 1) * C]
            tile = jnp.where(same, bwd_tiles[lag], jnp.zeros((), jnp.bfloat16))
            acc = acc + jnp.dot(tile, grads(j), preferred_element_type=jnp.float32)
        mgrad_out[s * C : (s + 1) * C, :] = acc


def filter_sums(ids_own, ids_src, src, grad):
    own = grad.shape[0]
    blocks = ids_src.shape[0] // C
    ids_rev = ids_src.reshape(blocks, C)[:, ::-1].reshape(1, blocks * C)
    ext = pl.pallas_call(
        filter_kernel,
        out_shape=jax.ShapeDtypeStruct((1, (MAXCH + 2) * C), jnp.float32),
        compiler_params=pltpu.CompilerParams(vmem_limit_bytes=40 * 1024 * 1024),
        interpret=INTERPRET,
    )(ids_own.reshape(own, 1), ids_rev, *src, grad)
    return ext[0, C - 1 : C - 1 + FLEN]


def local_conv(taps, ids_own, ids_src, ids_rdr, skip, src, grads):
    own, width = grads[0].shape
    lags = MAXCH + 1
    taps_row = jnp.pad(taps.astype(jnp.float32), (2 * C, 2 * C)).reshape(1, -1)
    return pl.pallas_call(
        conv_kernel,
        out_shape=(
            jax.ShapeDtypeStruct((own, width), jnp.float32),
            jax.ShapeDtypeStruct((own, width), jnp.float32),
        ),
        scratch_shapes=[pltpu.VMEM((lags, C, C), jnp.bfloat16), pltpu.VMEM((lags, C, C), jnp.bfloat16)],
        compiler_params=pltpu.CompilerParams(vmem_limit_bytes=60 * 1024 * 1024),
        interpret=INTERPRET,
    )(taps_row, ids_own.reshape(own, 1), ids_src.reshape(1, -1),
      ids_rdr.reshape(1, -1), skip.reshape(1, width), *src, *grads)


def shards(query_in, key_in, value_in, out_grad, doc_ids, skip_gain, filter_taps):
    rows, width = query_in.shape
    assert width == FGROUP and rows % C == 0
    here = lax.axis_index("ctx")
    span = -(-FLEN // rows)
    hist = span * rows
    assert hist == MAXCH * C

    count = lax.axis_size("ctx")
    groups = lax.axis_size("tp")
    pieces = lax.all_to_all(filter_taps, "tp", split_axis=1, concat_axis=0, tiled=True)
    taps = lax.all_to_all(jnp.tile(pieces, (count, 1)), "ctx", 0, 0, tiled=True).reshape(FLEN)

    mixed_in = (key_in.astype(jnp.float32) * value_in.astype(jnp.float32)).astype(jnp.bfloat16)
    conv_grad = (out_grad.astype(jnp.float32) * query_in.astype(jnp.float32)).astype(jnp.bfloat16)

    ahead = [mixed_in]
    behind = [conv_grad]
    for _ in range(span):
        ahead.append(shifted(ahead[-1], "ctx", 1))
        behind.append(shifted(behind[-1], "ctx", -1))

    ids_pad = jnp.concatenate(
        [jnp.full((hist,), -1, jnp.int32), doc_ids, jnp.full((hist,), -2, jnp.int32)]
    )
    ids_own = lax.dynamic_slice_in_dim(doc_ids, here * rows, rows)
    ids_src = lax.dynamic_slice_in_dim(ids_pad, here * rows, hist + rows)
    ids_rdr = lax.dynamic_slice_in_dim(ids_pad, here * rows + hist, hist + rows)

    filter_part = filter_sums(ids_own, ids_src, ahead[::-1], conv_grad)
    spread = lax.all_to_all(filter_part.reshape(count, FLEN // count), "ctx", 0, 0, tiled=True)
    block_sum = jnp.sum(spread, axis=0).reshape(groups, FLEN // (count * groups))
    conv, mixed_grad = local_conv(taps, ids_own, ids_src, ids_rdr, skip_gain, ahead[::-1], behind)

    mixed_out = (query_in.astype(jnp.float32) * conv).astype(jnp.bfloat16)
    query_grad = (out_grad.astype(jnp.float32) * conv).astype(jnp.bfloat16)
    key_grad = (mixed_grad * value_in.astype(jnp.float32)).astype(jnp.bfloat16)
    value_grad = (mixed_grad * key_in.astype(jnp.float32)).astype(jnp.bfloat16)

    summed = lax.all_to_all(block_sum, "tp", 0, 0, tiled=True).T
    tokens = lax.axis_size("ctx") * rows
    filter_grad = summed * (1.0 / math.sqrt(FGROUP * tokens))
    return (mixed_out, query_grad, key_grad, value_grad, filter_grad)


def solution(mesh):
    in_specs = (
        P("ctx", "tp"),
        P("ctx", "tp"),
        P("ctx", "tp"),
        P("ctx", "tp"),
        P(),
        P("tp"),
        P(("ctx", "tp"), None),
    )
    out_specs = (
        P("ctx", "tp"),
        P("ctx", "tp"),
        P("ctx", "tp"),
        P("ctx", "tp"),
        P(("ctx", "tp"), None),
    )
    return jax.shard_map(shards, mesh=mesh, in_specs=in_specs, out_specs=out_specs, check_vma=False)
```

```python
import math

import jax
import jax.numpy as jnp
from jax import lax
from jax.experimental import pallas as pl
from jax.experimental.pallas import tpu as pltpu
from jax.sharding import PartitionSpec as P

MAXCH = 8
FGROUP = 512
FLEN = 2048
C = 256
INTERPRET = False


def shifted(value, axis, steps):
    count = lax.axis_size(axis)
    leading, last = (max(0, -steps), min(count, count - steps))
    return lax.ppermute(value, axis, [(source, source + steps) for source in range(leading, last)])


def band_tiles(taps_row, fwd_tiles, bwd_tiles):
    for lag in range(MAXCH + 1):
        start = C * lag + C
        wide = jnp.broadcast_to(taps_row[:, start : start + 2 * C], (C, 2 * C))
        tile = pltpu.roll(wide, 0, 1, stride=1, stride_axis=0)[:, C:]
        bwd_tiles[lag] = tile.astype(jnp.bfloat16)
        fwd_tiles[lag] = tile.T.astype(jnp.bfloat16)


def filter_kernel(ids_own, ids_rev, *refs):
    lags = MAXCH + 1
    count = len(refs) - 2
    src_refs, grad_ref, filt_out = refs[:count], refs[count], refs[count + 1]
    own = grad_ref.shape[0]
    parts = own // C

    exchange = (lax.broadcasted_iota(jnp.int32, (C, C), 0) + lax.broadcasted_iota(jnp.int32, (C, C), 1)
                == C - 1).astype(jnp.bfloat16)
    flipped = {}

    def src_rev(j):
        if j not in flipped:
            block = src_refs[j // parts][(j % parts) * C : (j % parts + 1) * C, :]
            flipped[j] = jnp.dot(exchange, block, preferred_element_type=jnp.float32).astype(jnp.bfloat16)
        return flipped[j]

    sums = [jnp.zeros((1, 2 * C), jnp.float32) for _ in range(lags)]
    for r in range(parts):
        reader_ids = ids_own[r * C : (r + 1) * C, :]
        grad = grad_ref[r * C : (r + 1) * C, :]
        for j in range(MAXCH + parts):
            lag = MAXCH + r - j
            if not 0 <= lag <= MAXCH:
                continue
            prod = lax.dot_general(grad, src_rev(j), (((1,), (1,)), ((), ())),
                                   preferred_element_type=jnp.float32)
            prod = jnp.where(reader_ids == ids_rev[:, j * C : (j + 1) * C], prod, 0.0)
            wide = jnp.concatenate([prod, jnp.zeros((C, C), jnp.float32)], axis=1)
            wide = pltpu.roll(wide, 0, 1, stride=1, stride_axis=0)
            sums[lag] = sums[lag] + jnp.sum(wide, axis=0, keepdims=True)
    filt_out[...] = jnp.zeros(filt_out.shape, jnp.float32)
    for lag in range(lags):
        filt_out[:, C * lag : C * lag + 2 * C] += sums[lag]


def conv_kernel(taps_row, ids_own, ids_src, ids_rdr, skip, *refs):
    lags = MAXCH + 1
    count = (len(refs) - 4) // 2
    src_refs, grad_refs = refs[:count], refs[count : 2 * count]
    conv_out, mgrad_out, fwd_tiles, bwd_tiles = refs[2 * count :]
    own = src_refs[0].shape[0]
    parts = own // C

    def src(j):
        return src_refs[j // parts][(j % parts) * C : (j % parts + 1) * C, :]

    def grads(j):
        return grad_refs[j // parts][(j % parts) * C : (j % parts + 1) * C, :]

    band_tiles(taps_row, fwd_tiles, bwd_tiles)
    skip_row = skip[...]
    for r in range(parts):
        reader_ids = ids_own[r * C : (r + 1) * C, :]
        acc = skip_row * src(MAXCH + r).astype(jnp.float32)
        for j in range(MAXCH + parts):
            lag = MAXCH + r - j
            if not 0 <= lag <= MAXCH:
                continue
            same = reader_ids == ids_src[:, j * C : (j + 1) * C]
            tile = jnp.where(same, fwd_tiles[lag], jnp.zeros((), jnp.bfloat16))
            acc = acc + jnp.dot(tile, src(j), preferred_element_type=jnp.float32)
        conv_out[r * C : (r + 1) * C, :] = acc
    for s in range(parts):
        source_ids = ids_own[s * C : (s + 1) * C, :]
        acc = skip_row * grads(s).astype(jnp.float32)
        for lag in range(lags):
            j = s + lag
            same = source_ids == ids_rdr[:, j * C : (j + 1) * C]
            tile = jnp.where(same, bwd_tiles[lag], jnp.zeros((), jnp.bfloat16))
            acc = acc + jnp.dot(tile, grads(j), preferred_element_type=jnp.float32)
        mgrad_out[s * C : (s + 1) * C, :] = acc


def filter_sums(ids_own, ids_src, src, grad):
    own = grad.shape[0]
    blocks = ids_src.shape[0] // C
    ids_rev = ids_src.reshape(blocks, C)[:, ::-1].reshape(1, blocks * C)
    ext = pl.pallas_call(
        filter_kernel,
        out_shape=jax.ShapeDtypeStruct((1, (MAXCH + 2) * C), jnp.float32),
        compiler_params=pltpu.CompilerParams(vmem_limit_bytes=40 * 1024 * 1024),
        interpret=INTERPRET,
    )(ids_own.reshape(own, 1), ids_rev, *src, grad)
    return ext[0, C - 1 : C - 1 + FLEN]


def local_conv(taps, ids_own, ids_src, ids_rdr, skip, src, grads):
    own, width = grads[0].shape
    lags = MAXCH + 1
    taps_row = jnp.pad(taps.astype(jnp.float32), (2 * C, 2 * C)).reshape(1, -1)
    return pl.pallas_call(
        conv_kernel,
        out_shape=(
            jax.ShapeDtypeStruct((own, width), jnp.float32),
            jax.ShapeDtypeStruct((own, width), jnp.float32),
        ),
        scratch_shapes=[pltpu.VMEM((lags, C, C), jnp.bfloat16), pltpu.VMEM((lags, C, C), jnp.bfloat16)],
        compiler_params=pltpu.CompilerParams(vmem_limit_bytes=60 * 1024 * 1024),
        interpret=INTERPRET,
    )(taps_row, ids_own.reshape(own, 1), ids_src.reshape(1, -1),
      ids_rdr.reshape(1, -1), skip.reshape(1, width), *src, *grads)


def shards(query_in, key_in, value_in, out_grad, doc_ids, skip_gain, filter_taps):
    rows, width = query_in.shape
    assert width == FGROUP and rows % C == 0
    here = lax.axis_index("ctx")
    span = -(-FLEN // rows)
    hist = span * rows
    assert hist == MAXCH * C

    count = lax.axis_size("ctx")
    groups = lax.axis_size("tp")
    pieces = lax.all_to_all(filter_taps, "tp", split_axis=1, concat_axis=0, tiled=True)
    row = pieces.reshape(1, FLEN // count)
    taps = lax.all_to_all(jnp.tile(row, (count, 1)), "ctx", 0, 0, tiled=True).reshape(FLEN)

    mixed_in = (key_in.astype(jnp.float32) * value_in.astype(jnp.float32)).astype(jnp.bfloat16)
    conv_grad = (out_grad.astype(jnp.float32) * query_in.astype(jnp.float32)).astype(jnp.bfloat16)

    ahead = [mixed_in]
    behind = [conv_grad]
    for _ in range(span):
        ahead.append(shifted(ahead[-1], "ctx", 1))
        behind.append(shifted(behind[-1], "ctx", -1))

    ids_pad = jnp.concatenate(
        [jnp.full((hist,), -1, jnp.int32), doc_ids, jnp.full((hist,), -2, jnp.int32)]
    )
    ids_own = lax.dynamic_slice_in_dim(doc_ids, here * rows, rows)
    ids_src = lax.dynamic_slice_in_dim(ids_pad, here * rows, hist + rows)
    ids_rdr = lax.dynamic_slice_in_dim(ids_pad, here * rows + hist, hist + rows)

    filter_part = filter_sums(ids_own, ids_src, ahead[::-1], conv_grad)
    spread = lax.all_to_all(filter_part.reshape(count, FLEN // count), "ctx", 0, 0, tiled=True)
    block_sum = jnp.sum(spread, axis=0).reshape(groups, FLEN // (count * groups))
    conv, mixed_grad = local_conv(taps, ids_own, ids_src, ids_rdr, skip_gain, ahead[::-1], behind)

    mixed_out = (query_in.astype(jnp.float32) * conv).astype(jnp.bfloat16)
    query_grad = (out_grad.astype(jnp.float32) * conv).astype(jnp.bfloat16)
    key_grad = (mixed_grad * value_in.astype(jnp.float32)).astype(jnp.bfloat16)
    value_grad = (mixed_grad * key_in.astype(jnp.float32)).astype(jnp.bfloat16)

    summed = lax.all_to_all(block_sum, "tp", 0, 0, tiled=True).T
    tokens = lax.axis_size("ctx") * rows
    filter_grad = summed * (1.0 / math.sqrt(FGROUP * tokens))
    return (mixed_out, query_grad, key_grad, value_grad, filter_grad)


def solution(mesh):
    in_specs = (
        P("ctx", "tp"),
        P("ctx", "tp"),
        P("ctx", "tp"),
        P("ctx", "tp"),
        P(),
        P("tp"),
        P(("ctx", "tp"), None),
    )
    out_specs = (
        P("ctx", "tp"),
        P("ctx", "tp"),
        P("ctx", "tp"),
        P("ctx", "tp"),
        P(("ctx", "tp"), None),
    )
    return jax.shard_map(shards, mesh=mesh, in_specs=in_specs, out_specs=out_specs, check_vma=False)
```

```python
import math

import jax
import jax.numpy as jnp
from jax import lax
from jax.experimental import pallas as pl
from jax.experimental.pallas import tpu as pltpu
from jax.sharding import PartitionSpec as P

MAXCH = 8
FGROUP = 512
FLEN = 2048
C = 256
INTERPRET = False


def shifted(value, axis, steps):
    count = lax.axis_size(axis)
    leading, last = (max(0, -steps), min(count, count - steps))
    return lax.ppermute(value, axis, [(source, source + steps) for source in range(leading, last)])


def band_tiles(taps_row, fwd_tiles, bwd_tiles):
    for lag in range(MAXCH + 1):
        start = C * lag + C
        wide = jnp.broadcast_to(taps_row[:, start : start + 2 * C], (C, 2 * C))
        tile = pltpu.roll(wide, 0, 1, stride=1, stride_axis=0)[:, C:]
        bwd_tiles[lag] = tile.astype(jnp.bfloat16)
        fwd_tiles[lag] = tile.T.astype(jnp.bfloat16)


def filter_kernel(ids_own, ids_rev, *refs):
    lags = MAXCH + 1
    count = len(refs) - 2
    src_refs, grad_ref, filt_out = refs[:count], refs[count], refs[count + 1]
    own = grad_ref.shape[0]
    parts = own // C

    exchange = (lax.broadcasted_iota(jnp.int32, (C, C), 0) + lax.broadcasted_iota(jnp.int32, (C, C), 1)
                == C - 1).astype(jnp.bfloat16)
    flipped = {}

    def src_rev(j):
        if j not in flipped:
            block = src_refs[j // parts][(j % parts) * C : (j % parts + 1) * C, :]
            flipped[j] = jnp.dot(exchange, block, preferred_element_type=jnp.float32).astype(jnp.bfloat16)
        return flipped[j]

    sums = [jnp.zeros((1, 2 * C), jnp.float32) for _ in range(lags)]
    for r in range(parts):
        reader_ids = ids_own[r * C : (r + 1) * C, :]
        grad = grad_ref[r * C : (r + 1) * C, :]
        for j in range(MAXCH + parts):
            lag = MAXCH + r - j
            if not 0 <= lag <= MAXCH:
                continue
            prod = lax.dot_general(grad, src_rev(j), (((1,), (1,)), ((), ())),
                                   preferred_element_type=jnp.float32)
            prod = jnp.where(reader_ids == ids_rev[:, j * C : (j + 1) * C], prod, 0.0)
            wide = jnp.concatenate([prod, jnp.zeros((C, C), jnp.float32)], axis=1)
            wide = pltpu.roll(wide, 0, 1, stride=1, stride_axis=0)
            sums[lag] = sums[lag] + jnp.sum(wide, axis=0, keepdims=True)
    filt_out[...] = jnp.zeros(filt_out.shape, jnp.float32)
    for lag in range(lags):
        filt_out[:, C * lag : C * lag + 2 * C] += sums[lag]


def conv_kernel(taps_row, ids_own, ids_src, ids_rdr, skip, *refs):
    lags = MAXCH + 1
    count = (len(refs) - 4) // 2
    src_refs, grad_refs = refs[:count], refs[count : 2 * count]
    conv_out, mgrad_out, fwd_tiles, bwd_tiles = refs[2 * count :]
    own = src_refs[0].shape[0]
    parts = own // C

    def src(j):
        return src_refs[j // parts][(j % parts) * C : (j % parts + 1) * C, :]

    def grads(j):
        return grad_refs[j // parts][(j % parts) * C : (j % parts + 1) * C, :]

    band_tiles(taps_row, fwd_tiles, bwd_tiles)
    skip_row = skip[...]
    for r in range(parts):
        reader_ids = ids_own[r * C : (r + 1) * C, :]
        acc = skip_row * src(MAXCH + r).astype(jnp.float32)
        for j in range(MAXCH + parts):
            lag = MAXCH + r - j
            if not 0 <= lag <= MAXCH:
                continue
            same = reader_ids == ids_src[:, j * C : (j + 1) * C]
            tile = jnp.where(same, fwd_tiles[lag], jnp.zeros((), jnp.bfloat16))
            acc = acc + jnp.dot(tile, src(j), preferred_element_type=jnp.float32)
        conv_out[r * C : (r + 1) * C, :] = acc
    for s in range(parts):
        source_ids = ids_own[s * C : (s + 1) * C, :]
        acc = skip_row * grads(s).astype(jnp.float32)
        for lag in range(lags):
            j = s + lag
            same = source_ids == ids_rdr[:, j * C : (j + 1) * C]
            tile = jnp.where(same, bwd_tiles[lag], jnp.zeros((), jnp.bfloat16))
            acc = acc + jnp.dot(tile, grads(j), preferred_element_type=jnp.float32)
        mgrad_out[s * C : (s + 1) * C, :] = acc


def filter_sums(ids_own, ids_src, src, grad):
    own = grad.shape[0]
    blocks = ids_src.shape[0] // C
    ids_rev = ids_src.reshape(blocks, C)[:, ::-1].reshape(1, blocks * C)
    ext = pl.pallas_call(
        filter_kernel,
        out_shape=jax.ShapeDtypeStruct((1, (MAXCH + 2) * C), jnp.float32),
        compiler_params=pltpu.CompilerParams(vmem_limit_bytes=40 * 1024 * 1024),
        interpret=INTERPRET,
    )(ids_own.reshape(own, 1), ids_rev, *src, grad)
    return ext[0, C - 1 : C - 1 + FLEN]


def local_conv(taps, ids_own, ids_src, ids_rdr, skip, src, grads):
    own, width = grads[0].shape
    lags = MAXCH + 1
    taps_row = jnp.pad(taps.astype(jnp.float32), (2 * C, 2 * C)).reshape(1, -1)
    return pl.pallas_call(
        conv_kernel,
        out_shape=(
            jax.ShapeDtypeStruct((own, width), jnp.float32),
            jax.ShapeDtypeStruct((own, width), jnp.float32),
        ),
        scratch_shapes=[pltpu.VMEM((lags, C, C), jnp.bfloat16), pltpu.VMEM((lags, C, C), jnp.bfloat16)],
        compiler_params=pltpu.CompilerParams(vmem_limit_bytes=60 * 1024 * 1024),
        interpret=INTERPRET,
    )(taps_row, ids_own.reshape(own, 1), ids_src.reshape(1, -1),
      ids_rdr.reshape(1, -1), skip.reshape(1, width), *src, *grads)


def shards(query_in, key_in, value_in, out_grad, doc_ids, skip_gain, filter_taps):
    rows, width = query_in.shape
    assert width == FGROUP and rows % C == 0
    here = lax.axis_index("ctx")
    span = -(-FLEN // rows)
    hist = span * rows
    assert hist == MAXCH * C

    count = lax.axis_size("ctx")
    groups = lax.axis_size("tp")
    pieces = lax.all_to_all(filter_taps, "tp", split_axis=1, concat_axis=0, tiled=True)
    row = pieces.reshape(1, FLEN // count)
    taps = lax.all_to_all(jnp.tile(row, (count, 1)), "ctx", 0, 0, tiled=True).reshape(FLEN)

    mixed_in = (key_in.astype(jnp.float32) * value_in.astype(jnp.float32)).astype(jnp.bfloat16)
    conv_grad = (out_grad.astype(jnp.float32) * query_in.astype(jnp.float32)).astype(jnp.bfloat16)

    ahead = [mixed_in]
    behind = [conv_grad]
    for step in range(span):
        ahead.append(shifted(ahead[-1], "ctx", 1))
        behind.append(shifted(behind[-1], "ctx", -1))
        if step == 0:
            ahead[-1], behind[-1], taps = lax.optimization_barrier((ahead[-1], behind[-1], taps))

    ids_pad = jnp.concatenate(
        [jnp.full((hist,), -1, jnp.int32), doc_ids, jnp.full((hist,), -2, jnp.int32)]
    )
    ids_own = lax.dynamic_slice_in_dim(doc_ids, here * rows, rows)
    ids_src = lax.dynamic_slice_in_dim(ids_pad, here * rows, hist + rows)
    ids_rdr = lax.dynamic_slice_in_dim(ids_pad, here * rows + hist, hist + rows)

    filter_part = filter_sums(ids_own, ids_src, ahead[::-1], conv_grad)
    spread = lax.all_to_all(filter_part.reshape(count, FLEN // count), "ctx", 0, 0, tiled=True)
    block_sum = jnp.sum(spread, axis=0).reshape(groups, FLEN // (count * groups))
    conv, mixed_grad = local_conv(taps, ids_own, ids_src, ids_rdr, skip_gain, ahead[::-1], behind)

    mixed_out = (query_in.astype(jnp.float32) * conv).astype(jnp.bfloat16)
    query_grad = (out_grad.astype(jnp.float32) * conv).astype(jnp.bfloat16)
    key_grad = (mixed_grad * value_in.astype(jnp.float32)).astype(jnp.bfloat16)
    value_grad = (mixed_grad * key_in.astype(jnp.float32)).astype(jnp.bfloat16)

    summed = lax.all_to_all(block_sum, "tp", 0, 0, tiled=True).T
    tokens = lax.axis_size("ctx") * rows
    filter_grad = summed * (1.0 / math.sqrt(FGROUP * tokens))
    return (mixed_out, query_grad, key_grad, value_grad, filter_grad)


def solution(mesh):
    in_specs = (
        P("ctx", "tp"),
        P("ctx", "tp"),
        P("ctx", "tp"),
        P("ctx", "tp"),
        P(),
        P("tp"),
        P(("ctx", "tp"), None),
    )
    out_specs = (
        P("ctx", "tp"),
        P("ctx", "tp"),
        P("ctx", "tp"),
        P("ctx", "tp"),
        P(("ctx", "tp"), None),
    )
    return jax.shard_map(shards, mesh=mesh, in_specs=in_specs, out_specs=out_specs, check_vma=False)
```

```python
import math

import jax
import jax.numpy as jnp
from jax import lax
from jax.experimental import pallas as pl
from jax.experimental.pallas import tpu as pltpu
from jax.sharding import PartitionSpec as P

MAXCH = 8
FGROUP = 512
FLEN = 2048
C = 256
INTERPRET = False


def shifted(value, axis, steps):
    count = lax.axis_size(axis)
    leading, last = (max(0, -steps), min(count, count - steps))
    return lax.ppermute(value, axis, [(source, source + steps) for source in range(leading, last)])


def swapped(value, axis, bit):
    count = lax.axis_size(axis)
    return lax.ppermute(value, axis, [(source, source ^ bit) for source in range(count)])


def gather_chunks(chunk, axis):
    here = lax.axis_index(axis)
    count = lax.axis_size(axis)
    held = chunk
    bit = 1
    while bit < count:
        other = swapped(held, axis, bit)
        upper = (here & bit) != 0
        held = jnp.concatenate([jnp.where(upper, other, held), jnp.where(upper, held, other)])
        bit *= 2
    return held


def band_tiles(taps_row, fwd_tiles, bwd_tiles):
    for lag in range(MAXCH + 1):
        start = C * lag + C
        wide = jnp.broadcast_to(taps_row[:, start : start + 2 * C], (C, 2 * C))
        tile = pltpu.roll(wide, 0, 1, stride=1, stride_axis=0)[:, C:]
        bwd_tiles[lag] = tile.astype(jnp.bfloat16)
        fwd_tiles[lag] = tile.T.astype(jnp.bfloat16)


def filter_kernel(ids_own, ids_rev, *refs):
    lags = MAXCH + 1
    count = len(refs) - 2
    src_refs, grad_ref, filt_out = refs[:count], refs[count], refs[count + 1]
    own = grad_ref.shape[0]
    parts = own // C

    exchange = (lax.broadcasted_iota(jnp.int32, (C, C), 0) + lax.broadcasted_iota(jnp.int32, (C, C), 1)
                == C - 1).astype(jnp.bfloat16)
    flipped = {}

    def src_rev(j):
        if j not in flipped:
            block = src_refs[j // parts][(j % parts) * C : (j % parts + 1) * C, :]
            flipped[j] = jnp.dot(exchange, block, preferred_element_type=jnp.float32).astype(jnp.bfloat16)
        return flipped[j]

    sums = [jnp.zeros((1, 2 * C), jnp.float32) for _ in range(lags)]
    for r in range(parts):
        reader_ids = ids_own[r * C : (r + 1) * C, :]
        grad = grad_ref[r * C : (r + 1) * C, :]
        for j in range(MAXCH + parts):
            lag = MAXCH + r - j
            if not 0 <= lag <= MAXCH:
                continue
            prod = lax.dot_general(grad, src_rev(j), (((1,), (1,)), ((), ())),
                                   preferred_element_type=jnp.float32)
            prod = jnp.where(reader_ids == ids_rev[:, j * C : (j + 1) * C], prod, 0.0)
            wide = jnp.concatenate([prod, jnp.zeros((C, C), jnp.float32)], axis=1)
            wide = pltpu.roll(wide, 0, 1, stride=1, stride_axis=0)
            sums[lag] = sums[lag] + jnp.sum(wide, axis=0, keepdims=True)
    filt_out[...] = jnp.zeros(filt_out.shape, jnp.float32)
    for lag in range(lags):
        filt_out[:, C * lag : C * lag + 2 * C] += sums[lag]


def conv_kernel(taps_row, ids_own, ids_src, ids_rdr, skip, *refs):
    lags = MAXCH + 1
    count = (len(refs) - 4) // 2
    src_refs, grad_refs = refs[:count], refs[count : 2 * count]
    conv_out, mgrad_out, fwd_tiles, bwd_tiles = refs[2 * count :]
    own = src_refs[0].shape[0]
    parts = own // C

    def src(j):
        return src_refs[j // parts][(j % parts) * C : (j % parts + 1) * C, :]

    def grads(j):
        return grad_refs[j // parts][(j % parts) * C : (j % parts + 1) * C, :]

    band_tiles(taps_row, fwd_tiles, bwd_tiles)
    skip_row = skip[...]
    for r in range(parts):
        reader_ids = ids_own[r * C : (r + 1) * C, :]
        acc = skip_row * src(MAXCH + r).astype(jnp.float32)
        for j in range(MAXCH + parts):
            lag = MAXCH + r - j
            if not 0 <= lag <= MAXCH:
                continue
            same = reader_ids == ids_src[:, j * C : (j + 1) * C]
            tile = jnp.where(same, fwd_tiles[lag], jnp.zeros((), jnp.bfloat16))
            acc = acc + jnp.dot(tile, src(j), preferred_element_type=jnp.float32)
        conv_out[r * C : (r + 1) * C, :] = acc
    for s in range(parts):
        source_ids = ids_own[s * C : (s + 1) * C, :]
        acc = skip_row * grads(s).astype(jnp.float32)
        for lag in range(lags):
            j = s + lag
            same = source_ids == ids_rdr[:, j * C : (j + 1) * C]
            tile = jnp.where(same, bwd_tiles[lag], jnp.zeros((), jnp.bfloat16))
            acc = acc + jnp.dot(tile, grads(j), preferred_element_type=jnp.float32)
        mgrad_out[s * C : (s + 1) * C, :] = acc


def filter_sums(ids_own, ids_src, src, grad):
    own = grad.shape[0]
    blocks = ids_src.shape[0] // C
    ids_rev = ids_src.reshape(blocks, C)[:, ::-1].reshape(1, blocks * C)
    ext = pl.pallas_call(
        filter_kernel,
        out_shape=jax.ShapeDtypeStruct((1, (MAXCH + 2) * C), jnp.float32),
        compiler_params=pltpu.CompilerParams(vmem_limit_bytes=40 * 1024 * 1024),
        interpret=INTERPRET,
    )(ids_own.reshape(own, 1), ids_rev, *src, grad)
    return ext[0, C - 1 : C - 1 + FLEN]


def local_conv(taps, ids_own, ids_src, ids_rdr, skip, src, grads):
    own, width = grads[0].shape
    lags = MAXCH + 1
    taps_row = jnp.pad(taps.astype(jnp.float32), (2 * C, 2 * C)).reshape(1, -1)
    return pl.pallas_call(
        conv_kernel,
        out_shape=(
            jax.ShapeDtypeStruct((own, width), jnp.float32),
            jax.ShapeDtypeStruct((own, width), jnp.float32),
        ),
        scratch_shapes=[pltpu.VMEM((lags, C, C), jnp.bfloat16), pltpu.VMEM((lags, C, C), jnp.bfloat16)],
        compiler_params=pltpu.CompilerParams(vmem_limit_bytes=60 * 1024 * 1024),
        interpret=INTERPRET,
    )(taps_row, ids_own.reshape(own, 1), ids_src.reshape(1, -1),
      ids_rdr.reshape(1, -1), skip.reshape(1, width), *src, *grads)


def shards(query_in, key_in, value_in, out_grad, doc_ids, skip_gain, filter_taps):
    rows, width = query_in.shape
    assert width == FGROUP and rows % C == 0
    here = lax.axis_index("ctx")
    span = -(-FLEN // rows)
    hist = span * rows
    assert hist == MAXCH * C

    count = lax.axis_size("ctx")
    groups = lax.axis_size("tp")
    block = gather_chunks(filter_taps, "tp")
    own_filter = lax.dynamic_slice_in_dim(block, lax.axis_index("tp"), 1, axis=1)[:, 0]
    taps = gather_chunks(own_filter, "ctx")

    mixed_in = (key_in.astype(jnp.float32) * value_in.astype(jnp.float32)).astype(jnp.bfloat16)
    conv_grad = (out_grad.astype(jnp.float32) * query_in.astype(jnp.float32)).astype(jnp.bfloat16)

    ahead = [mixed_in]
    behind = [conv_grad]
    for _ in range(span):
        ahead.append(shifted(ahead[-1], "ctx", 1))
        behind.append(shifted(behind[-1], "ctx", -1))

    ids_pad = jnp.concatenate(
        [jnp.full((hist,), -1, jnp.int32), doc_ids, jnp.full((hist,), -2, jnp.int32)]
    )
    ids_own = lax.dynamic_slice_in_dim(doc_ids, here * rows, rows)
    ids_src = lax.dynamic_slice_in_dim(ids_pad, here * rows, hist + rows)
    ids_rdr = lax.dynamic_slice_in_dim(ids_pad, here * rows + hist, hist + rows)

    filter_part = filter_sums(ids_own, ids_src, ahead[::-1], conv_grad)
    spread = lax.all_to_all(filter_part.reshape(count, FLEN // count), "ctx", 0, 0, tiled=True)
    block_sum = jnp.sum(spread, axis=0).reshape(groups, FLEN // (count * groups))
    conv, mixed_grad = local_conv(taps, ids_own, ids_src, ids_rdr, skip_gain, ahead[::-1], behind)

    mixed_out = (query_in.astype(jnp.float32) * conv).astype(jnp.bfloat16)
    query_grad = (out_grad.astype(jnp.float32) * conv).astype(jnp.bfloat16)
    key_grad = (mixed_grad * value_in.astype(jnp.float32)).astype(jnp.bfloat16)
    value_grad = (mixed_grad * key_in.astype(jnp.float32)).astype(jnp.bfloat16)

    summed = lax.all_to_all(block_sum, "tp", 0, 0, tiled=True).T
    tokens = lax.axis_size("ctx") * rows
    filter_grad = summed * (1.0 / math.sqrt(FGROUP * tokens))
    return (mixed_out, query_grad, key_grad, value_grad, filter_grad)


def solution(mesh):
    in_specs = (
        P("ctx", "tp"),
        P("ctx", "tp"),
        P("ctx", "tp"),
        P("ctx", "tp"),
        P(),
        P("tp"),
        P(("ctx", "tp"), None),
    )
    out_specs = (
        P("ctx", "tp"),
        P("ctx", "tp"),
        P("ctx", "tp"),
        P("ctx", "tp"),
        P(("ctx", "tp"), None),
    )
    return jax.shard_map(shards, mesh=mesh, in_specs=in_specs, out_specs=out_specs, check_vma=False)
```

```python
import math

import jax
import jax.numpy as jnp
from jax import lax
from jax.experimental import pallas as pl
from jax.experimental.pallas import tpu as pltpu
from jax.sharding import PartitionSpec as P

MAXCH = 8
FGROUP = 512
FLEN = 2048
C = 256
INTERPRET = False


def shifted(value, axis, steps):
    count = lax.axis_size(axis)
    leading, last = (max(0, -steps), min(count, count - steps))
    return lax.ppermute(value, axis, [(source, source + steps) for source in range(leading, last)])


def swapped(value, axis, bit):
    count = lax.axis_size(axis)
    return lax.ppermute(value, axis, [(source, source ^ bit) for source in range(count)])


def gather_chunks(chunk, axis):
    here = lax.axis_index(axis)
    count = lax.axis_size(axis)
    held = chunk
    bit = 1
    while bit < count:
        other = swapped(held, axis, bit)
        upper = (here & bit) != 0
        held = jnp.concatenate([jnp.where(upper, other, held), jnp.where(upper, held, other)])
        bit *= 2
    return held


def band_tiles(taps_row, fwd_tiles, bwd_tiles):
    for lag in range(MAXCH + 1):
        start = C * lag + C
        wide = jnp.broadcast_to(taps_row[:, start : start + 2 * C], (C, 2 * C))
        tile = pltpu.roll(wide, 0, 1, stride=1, stride_axis=0)[:, C:]
        bwd_tiles[lag] = tile.astype(jnp.bfloat16)
        fwd_tiles[lag] = tile.T.astype(jnp.bfloat16)


def filter_kernel(ids_own, ids_rev, *refs):
    lags = MAXCH + 1
    count = len(refs) - 2
    src_refs, grad_ref, filt_out = refs[:count], refs[count], refs[count + 1]
    own = grad_ref.shape[0]
    parts = own // C

    exchange = (lax.broadcasted_iota(jnp.int32, (C, C), 0) + lax.broadcasted_iota(jnp.int32, (C, C), 1)
                == C - 1).astype(jnp.bfloat16)
    flipped = {}

    def src_rev(j):
        if j not in flipped:
            block = src_refs[j // parts][(j % parts) * C : (j % parts + 1) * C, :]
            flipped[j] = jnp.dot(exchange, block, preferred_element_type=jnp.float32).astype(jnp.bfloat16)
        return flipped[j]

    sums = [jnp.zeros((1, 2 * C), jnp.float32) for _ in range(lags)]
    for r in range(parts):
        reader_ids = ids_own[r * C : (r + 1) * C, :]
        grad = grad_ref[r * C : (r + 1) * C, :]
        for j in range(MAXCH + parts):
            lag = MAXCH + r - j
            if not 0 <= lag <= MAXCH:
                continue
            prod = lax.dot_general(grad, src_rev(j), (((1,), (1,)), ((), ())),
                                   preferred_element_type=jnp.float32)
            prod = jnp.where(reader_ids == ids_rev[:, j * C : (j + 1) * C], prod, 0.0)
            wide = jnp.concatenate([prod, jnp.zeros((C, C), jnp.float32)], axis=1)
            wide = pltpu.roll(wide, 0, 1, stride=1, stride_axis=0)
            sums[lag] = sums[lag] + jnp.sum(wide, axis=0, keepdims=True)
    filt_out[...] = jnp.zeros(filt_out.shape, jnp.float32)
    for lag in range(lags):
        filt_out[:, C * lag : C * lag + 2 * C] += sums[lag]


def conv_kernel(taps_row, ids_own, ids_src, ids_rdr, skip, *refs):
    lags = MAXCH + 1
    count = (len(refs) - 4) // 2
    src_refs, grad_refs = refs[:count], refs[count : 2 * count]
    conv_out, mgrad_out, fwd_tiles, bwd_tiles = refs[2 * count :]
    own = src_refs[0].shape[0]
    parts = own // C

    def src(j):
        return src_refs[j // parts][(j % parts) * C : (j % parts + 1) * C, :]

    def grads(j):
        return grad_refs[j // parts][(j % parts) * C : (j % parts + 1) * C, :]

    band_tiles(taps_row, fwd_tiles, bwd_tiles)
    skip_row = skip[...]
    for r in range(parts):
        reader_ids = ids_own[r * C : (r + 1) * C, :]
        acc = skip_row * src(MAXCH + r).astype(jnp.float32)
        for j in range(MAXCH + parts):
            lag = MAXCH + r - j
            if not 0 <= lag <= MAXCH:
                continue
            same = reader_ids == ids_src[:, j * C : (j + 1) * C]
            tile = jnp.where(same, fwd_tiles[lag], jnp.zeros((), jnp.bfloat16))
            acc = acc + jnp.dot(tile, src(j), preferred_element_type=jnp.float32)
        conv_out[r * C : (r + 1) * C, :] = acc
    for s in range(parts):
        source_ids = ids_own[s * C : (s + 1) * C, :]
        acc = skip_row * grads(s).astype(jnp.float32)
        for lag in range(lags):
            j = s + lag
            same = source_ids == ids_rdr[:, j * C : (j + 1) * C]
            tile = jnp.where(same, bwd_tiles[lag], jnp.zeros((), jnp.bfloat16))
            acc = acc + jnp.dot(tile, grads(j), preferred_element_type=jnp.float32)
        mgrad_out[s * C : (s + 1) * C, :] = acc


def filter_sums(ids_own, ids_src, src, grad):
    own = grad.shape[0]
    blocks = ids_src.shape[0] // C
    ids_rev = ids_src.reshape(blocks, C)[:, ::-1].reshape(1, blocks * C)
    ext = pl.pallas_call(
        filter_kernel,
        out_shape=jax.ShapeDtypeStruct((1, (MAXCH + 2) * C), jnp.float32),
        compiler_params=pltpu.CompilerParams(vmem_limit_bytes=40 * 1024 * 1024),
        interpret=INTERPRET,
    )(ids_own.reshape(own, 1), ids_rev, *src, grad)
    return ext[0, C - 1 : C - 1 + FLEN]


def local_conv(taps, ids_own, ids_src, ids_rdr, skip, src, grads):
    own, width = grads[0].shape
    lags = MAXCH + 1
    taps_row = jnp.pad(taps.astype(jnp.float32), (2 * C, 2 * C)).reshape(1, -1)
    return pl.pallas_call(
        conv_kernel,
        out_shape=(
            jax.ShapeDtypeStruct((own, width), jnp.float32),
            jax.ShapeDtypeStruct((own, width), jnp.float32),
        ),
        scratch_shapes=[pltpu.VMEM((lags, C, C), jnp.bfloat16), pltpu.VMEM((lags, C, C), jnp.bfloat16)],
        compiler_params=pltpu.CompilerParams(vmem_limit_bytes=60 * 1024 * 1024),
        interpret=INTERPRET,
    )(taps_row, ids_own.reshape(own, 1), ids_src.reshape(1, -1),
      ids_rdr.reshape(1, -1), skip.reshape(1, width), *src, *grads)


def shards(query_in, key_in, value_in, out_grad, doc_ids, skip_gain, filter_taps):
    rows, width = query_in.shape
    assert width == FGROUP and rows % C == 0
    here = lax.axis_index("ctx")
    span = -(-FLEN // rows)
    hist = span * rows
    assert hist == MAXCH * C

    count = lax.axis_size("ctx")
    groups = lax.axis_size("tp")
    block = gather_chunks(filter_taps, "tp")
    own_filter = lax.dynamic_slice_in_dim(block, lax.axis_index("tp"), 1, axis=1)[:, 0]
    taps = gather_chunks(own_filter, "ctx")

    mixed_in = (key_in.astype(jnp.float32) * value_in.astype(jnp.float32)).astype(jnp.bfloat16)
    conv_grad = (out_grad.astype(jnp.float32) * query_in.astype(jnp.float32)).astype(jnp.bfloat16)

    ahead = [mixed_in]
    behind = [conv_grad]
    for _ in range(span):
        ahead.append(shifted(ahead[-1], "ctx", 1))
        behind.append(shifted(behind[-1], "ctx", -1))

    ids_pad = jnp.concatenate(
        [jnp.full((hist,), -1, jnp.int32), doc_ids, jnp.full((hist,), -2, jnp.int32)]
    )
    ids_own = lax.dynamic_slice_in_dim(doc_ids, here * rows, rows)
    ids_src = lax.dynamic_slice_in_dim(ids_pad, here * rows, hist + rows)
    ids_rdr = lax.dynamic_slice_in_dim(ids_pad, here * rows + hist, hist + rows)

    filter_part = filter_sums(ids_own, ids_src, ahead[::-1], conv_grad)
    every = ("ctx", "tp")
    devices = lax.axis_size(every)
    spread = lax.all_to_all(filter_part.reshape(devices, FLEN // devices), every, 0, 0, tiled=True)
    conv, mixed_grad = local_conv(taps, ids_own, ids_src, ids_rdr, skip_gain, ahead[::-1], behind)

    mixed_out = (query_in.astype(jnp.float32) * conv).astype(jnp.bfloat16)
    query_grad = (out_grad.astype(jnp.float32) * conv).astype(jnp.bfloat16)
    key_grad = (mixed_grad * value_in.astype(jnp.float32)).astype(jnp.bfloat16)
    value_grad = (mixed_grad * key_in.astype(jnp.float32)).astype(jnp.bfloat16)

    summed = jnp.sum(spread.reshape(devices // groups, groups, FLEN // devices), axis=0).T
    tokens = lax.axis_size("ctx") * rows
    filter_grad = summed * (1.0 / math.sqrt(FGROUP * tokens))
    return (mixed_out, query_grad, key_grad, value_grad, filter_grad)


def solution(mesh):
    in_specs = (
        P("ctx", "tp"),
        P("ctx", "tp"),
        P("ctx", "tp"),
        P("ctx", "tp"),
        P(),
        P("tp"),
        P(("ctx", "tp"), None),
    )
    out_specs = (
        P("ctx", "tp"),
        P("ctx", "tp"),
        P("ctx", "tp"),
        P("ctx", "tp"),
        P(("ctx", "tp"), None),
    )
    return jax.shard_map(shards, mesh=mesh, in_specs=in_specs, out_specs=out_specs, check_vma=False)
```

```python
import math

import jax
import jax.numpy as jnp
from jax import lax
from jax.experimental import pallas as pl
from jax.experimental.pallas import tpu as pltpu
from jax.sharding import PartitionSpec as P

MAXCH = 8
FGROUP = 512
FLEN = 2048
C = 256
INTERPRET = False


def shifted(value, axis, steps):
    count = lax.axis_size(axis)
    leading, last = (max(0, -steps), min(count, count - steps))
    return lax.ppermute(value, axis, [(source, source + steps) for source in range(leading, last)])


def swapped(value, axis, bit):
    count = lax.axis_size(axis)
    return lax.ppermute(value, axis, [(source, source ^ bit) for source in range(count)])


def gather_chunks(chunk, axis):
    here = lax.axis_index(axis)
    count = lax.axis_size(axis)
    held = chunk
    bit = 1
    while bit < count:
        other = swapped(held, axis, bit)
        upper = (here & bit) != 0
        held = jnp.concatenate([jnp.where(upper, other, held), jnp.where(upper, held, other)])
        bit *= 2
    return held


def band_tiles(taps_row, fwd_tiles, bwd_tiles):
    for lag in range(MAXCH + 1):
        start = C * lag + C
        wide = jnp.broadcast_to(taps_row[:, start : start + 2 * C], (C, 2 * C))
        tile = pltpu.roll(wide, 0, 1, stride=1, stride_axis=0)[:, C:]
        bwd_tiles[lag] = tile.astype(jnp.bfloat16)
        fwd_tiles[lag] = tile.T.astype(jnp.bfloat16)


def filter_kernel(ids_own, ids_rev, *refs):
    lags = MAXCH + 1
    count = len(refs) - 2
    src_refs, grad_ref, filt_out = refs[:count], refs[count], refs[count + 1]
    own = grad_ref.shape[0]
    parts = own // C

    exchange = (lax.broadcasted_iota(jnp.int32, (C, C), 0) + lax.broadcasted_iota(jnp.int32, (C, C), 1)
                == C - 1).astype(jnp.bfloat16)
    flipped = {}

    def src_rev(j):
        if j not in flipped:
            block = src_refs[j // parts][(j % parts) * C : (j % parts + 1) * C, :]
            flipped[j] = jnp.dot(exchange, block, preferred_element_type=jnp.float32).astype(jnp.bfloat16)
        return flipped[j]

    sums = [jnp.zeros((1, 2 * C), jnp.float32) for _ in range(lags)]
    for r in range(parts):
        reader_ids = ids_own[r * C : (r + 1) * C, :]
        grad = grad_ref[r * C : (r + 1) * C, :]
        for j in range(MAXCH + parts):
            lag = MAXCH + r - j
            if not 0 <= lag <= MAXCH:
                continue
            prod = lax.dot_general(grad, src_rev(j), (((1,), (1,)), ((), ())),
                                   preferred_element_type=jnp.float32)
            prod = jnp.where(reader_ids == ids_rev[:, j * C : (j + 1) * C], prod, 0.0)
            wide = jnp.concatenate([prod, jnp.zeros((C, C), jnp.float32)], axis=1)
            wide = pltpu.roll(wide, 0, 1, stride=1, stride_axis=0)
            sums[lag] = sums[lag] + jnp.sum(wide, axis=0, keepdims=True)
    filt_out[...] = jnp.zeros(filt_out.shape, jnp.float32)
    for lag in range(lags):
        filt_out[:, C * lag : C * lag + 2 * C] += sums[lag]


def conv_kernel(taps_row, ids_own, ids_src, ids_rdr, skip, *refs):
    lags = MAXCH + 1
    count = (len(refs) - 4) // 2
    src_refs, grad_refs = refs[:count], refs[count : 2 * count]
    conv_out, mgrad_out, fwd_tiles, bwd_tiles = refs[2 * count :]
    own = src_refs[0].shape[0]
    parts = own // C

    def src(j):
        return src_refs[j // parts][(j % parts) * C : (j % parts + 1) * C, :]

    def grads(j):
        return grad_refs[j // parts][(j % parts) * C : (j % parts + 1) * C, :]

    band_tiles(taps_row, fwd_tiles, bwd_tiles)
    skip_row = skip[...]
    for r in range(parts):
        reader_ids = ids_own[r * C : (r + 1) * C, :]
        acc = skip_row * src(MAXCH + r).astype(jnp.float32)
        for j in range(MAXCH + parts):
            lag = MAXCH + r - j
            if not 0 <= lag <= MAXCH:
                continue
            same = reader_ids == ids_src[:, j * C : (j + 1) * C]
            tile = jnp.where(same, fwd_tiles[lag], jnp.zeros((), jnp.bfloat16))
            acc = acc + jnp.dot(tile, src(j), preferred_element_type=jnp.float32)
        conv_out[r * C : (r + 1) * C, :] = acc
    for s in range(parts):
        source_ids = ids_own[s * C : (s + 1) * C, :]
        acc = skip_row * grads(s).astype(jnp.float32)
        for lag in range(lags):
            j = s + lag
            same = source_ids == ids_rdr[:, j * C : (j + 1) * C]
            tile = jnp.where(same, bwd_tiles[lag], jnp.zeros((), jnp.bfloat16))
            acc = acc + jnp.dot(tile, grads(j), preferred_element_type=jnp.float32)
        mgrad_out[s * C : (s + 1) * C, :] = acc


def filter_sums(ids_own, ids_src, src, grad):
    own = grad.shape[0]
    blocks = ids_src.shape[0] // C
    ids_rev = ids_src.reshape(blocks, C)[:, ::-1].reshape(1, blocks * C)
    ext = pl.pallas_call(
        filter_kernel,
        out_shape=jax.ShapeDtypeStruct((1, (MAXCH + 2) * C), jnp.float32),
        compiler_params=pltpu.CompilerParams(vmem_limit_bytes=40 * 1024 * 1024),
        interpret=INTERPRET,
    )(ids_own.reshape(own, 1), ids_rev, *src, grad)
    return ext[0, C - 1 : C - 1 + FLEN]


def local_conv(taps, ids_own, ids_src, ids_rdr, skip, src, grads):
    own, width = grads[0].shape
    lags = MAXCH + 1
    taps_row = jnp.pad(taps.astype(jnp.float32), (2 * C, 2 * C)).reshape(1, -1)
    return pl.pallas_call(
        conv_kernel,
        out_shape=(
            jax.ShapeDtypeStruct((own, width), jnp.float32),
            jax.ShapeDtypeStruct((own, width), jnp.float32),
        ),
        scratch_shapes=[pltpu.VMEM((lags, C, C), jnp.bfloat16), pltpu.VMEM((lags, C, C), jnp.bfloat16)],
        compiler_params=pltpu.CompilerParams(vmem_limit_bytes=60 * 1024 * 1024),
        interpret=INTERPRET,
    )(taps_row, ids_own.reshape(own, 1), ids_src.reshape(1, -1),
      ids_rdr.reshape(1, -1), skip.reshape(1, width), *src, *grads)


def shards(query_in, key_in, value_in, out_grad, doc_ids, skip_gain, filter_taps):
    rows, width = query_in.shape
    assert width == FGROUP and rows % C == 0
    here = lax.axis_index("ctx")
    span = -(-FLEN // rows)
    hist = span * rows
    assert hist == MAXCH * C

    count = lax.axis_size("ctx")
    groups = lax.axis_size("tp")
    block = gather_chunks(filter_taps, "tp")
    own_filter = lax.dynamic_slice_in_dim(block, lax.axis_index("tp"), 1, axis=1)[:, 0]
    taps = gather_chunks(own_filter, "ctx")

    mixed_in = (key_in.astype(jnp.float32) * value_in.astype(jnp.float32)).astype(jnp.bfloat16)
    conv_grad = (out_grad.astype(jnp.float32) * query_in.astype(jnp.float32)).astype(jnp.bfloat16)

    ahead = [mixed_in]
    behind = [conv_grad]
    for _ in range(span):
        ahead.append(shifted(ahead[-1], "ctx", 1))
        behind.append(shifted(behind[-1], "ctx", -1))

    ids_pad = jnp.concatenate(
        [jnp.full((hist,), -1, jnp.int32), doc_ids, jnp.full((hist,), -2, jnp.int32)]
    )
    ids_own = lax.dynamic_slice_in_dim(doc_ids, here * rows, rows)
    ids_src = lax.dynamic_slice_in_dim(ids_pad, here * rows, hist + rows)
    ids_rdr = lax.dynamic_slice_in_dim(ids_pad, here * rows + hist, hist + rows)

    filter_part = filter_sums(ids_own, ids_src, ahead[::-1], conv_grad)
    conv, mixed_grad = local_conv(taps, ids_own, ids_src, ids_rdr, skip_gain, ahead[::-1], behind)
    filter_part, conv, mixed_grad = lax.optimization_barrier((filter_part, conv, mixed_grad))
    spread = lax.all_to_all(filter_part.reshape(count, FLEN // count), "ctx", 0, 0, tiled=True)
    block_sum = jnp.sum(spread, axis=0).reshape(groups, FLEN // (count * groups))

    mixed_out = (query_in.astype(jnp.float32) * conv).astype(jnp.bfloat16)
    query_grad = (out_grad.astype(jnp.float32) * conv).astype(jnp.bfloat16)
    key_grad = (mixed_grad * value_in.astype(jnp.float32)).astype(jnp.bfloat16)
    value_grad = (mixed_grad * key_in.astype(jnp.float32)).astype(jnp.bfloat16)

    summed = lax.all_to_all(block_sum, "tp", 0, 0, tiled=True).T
    tokens = lax.axis_size("ctx") * rows
    filter_grad = summed * (1.0 / math.sqrt(FGROUP * tokens))
    return (mixed_out, query_grad, key_grad, value_grad, filter_grad)


def solution(mesh):
    in_specs = (
        P("ctx", "tp"),
        P("ctx", "tp"),
        P("ctx", "tp"),
        P("ctx", "tp"),
        P(),
        P("tp"),
        P(("ctx", "tp"), None),
    )
    out_specs = (
        P("ctx", "tp"),
        P("ctx", "tp"),
        P("ctx", "tp"),
        P("ctx", "tp"),
        P(("ctx", "tp"), None),
    )
    return jax.shard_map(shards, mesh=mesh, in_specs=in_specs, out_specs=out_specs, check_vma=False)
```
